32 devices in a mesh: section: 4 (over y, core), tensor: 8 (over z, x).
Axes of the slice: x: 2, y: 2, z: 4, core: 2. Of those that a mesh axis runs over, the one named last changes fastest.
Arguments:
- stream: bfloat16 [512, 2, 8192], P(None, None, 'section')
- concept_mean: bfloat16 [8192], P('section'), may hold values from -4 to 4
- erase_basis: bfloat16 [8192, 64], P('section'), may hold values from -0.0625 to 0.0625
- erase_lift: bfloat16 [8192, 64], P('section'), may hold values from -0.75 to 0.75
- norm_gain: float32 [8192], P('section'), may hold values from 0.1 to 1.9
- gate_weight: bfloat16 [8192, 28672], P('section', 'tensor'), may hold values from -0.0625 to 0.0625
- up_weight: bfloat16 [8192, 28672], P('section', 'tensor'), may hold values from -0.0625 to 0.0625
- down_weight: bfloat16 [28672, 8192], P('tensor', 'section'), may hold values from -0.03125 to 0.03125
Outputs:
- layer_out: bfloat16 [512, 2, 8192], P('tensor', None, 'section')
The draws below stay inside these ranges and needn't reach their ends.
All inputs are finite; a program needn't handle non-finite values.
Results may differ from the reference program's by a relative error of at most 0.015.
Values may be sent and summed in bfloat16 or wider, within the bound.
No kernel may reach another device: no remote copies, remote signals or barrier semaphores. Data moves between devices by JAX's collectives and lax.ppermute only.
A program may use at most 192 MiB of HBM per device.

```python
import jax
import jax.numpy as jnp
from jax import lax

D = 8192
FF = 28672
RANK = 64
MB = 2
SEQ = 512
TOKENS = 1024
N_SECTION = 4
N_TENSOR = 8


def draw_stream(key, part):
    first_key, second_key, third_key = jax.random.split(key, 3)
    position = jnp.arange(D, dtype=jnp.float32) / D
    column_scale = 0.4 * 10.0 ** (jax.random.uniform(second_key, (D,), jnp.float32) - 0.5) * 3.0 ** (position - 0.5)
    base_draw = jnp.clip(jax.random.normal(first_key, (SEQ, MB, D), jnp.float32), -4.0, 4.0)
    row_scale = 10.0 ** jax.random.uniform(third_key, (SEQ, MB, 1), jnp.float32, -0.4, 0.4)
    return (base_draw * row_scale * column_scale[None, None, :]).astype(jnp.bfloat16)


def levels(rng, shape, cuts, least, top_value):
    gain = 1.0
    for dim, blocks in cuts:
        draws = jax.random.uniform(jax.random.fold_in(jax.random.fold_in(rng, 6), dim), (blocks,), jnp.float32, least / len(cuts), top_value / len(cuts))
        gain = gain * jnp.repeat(jnp.exp(draws), shape[dim] // blocks).reshape((-1,) + (1,) * (len(shape) - 1 - dim))
    return gain


def centred(own_key, shape, deviation, bound, cuts=(), held_as=jnp.bfloat16):
    level = levels(own_key, shape, cuts, -0.22, 0.18) if cuts else 1.0
    entries = jax.random.normal(own_key, shape, jnp.float32) * deviation * level
    return jnp.minimum(jnp.maximum(entries, -bound), bound).astype(held_as)


def setup_inputs(seed: int = 0) -> dict:
    keys = jax.random.split(jax.random.key(seed), 9)
    stream = draw_stream(jax.random.fold_in(keys[8], 71), 0)
    concept_mean = centred(keys[1], (D,), 1.0, 4.0, ((0, 4),))
    erase_basis = centred(keys[2], (D, RANK), D ** -0.5, 0.0625, ((0, 4),))
    erase_lift = centred(keys[3], (D, RANK), RANK ** -0.5, 0.75, ((0, 4),))
    norm_gain = jnp.clip(1.0 + 0.18 * jax.random.normal(keys[4], (D,), jnp.float32), 0.1, 1.9)
    gate_weight = centred(keys[5], (D, FF), D ** -0.5, 0.0625, ((0, 4), (1, 8)))
    up_weight = centred(keys[6], (D, FF), D ** -0.5, 0.0625, ((0, 4), (1, 8)))
    down_weight = centred(keys[7], (FF, D), FF ** -0.5, 0.03125, ((0, 8), (1, 4)))
    return {"stream": stream, "concept_mean": concept_mean, "erase_basis": erase_basis, "erase_lift": erase_lift, "norm_gain": norm_gain, "gate_weight": gate_weight, "up_weight": up_weight, "down_weight": down_weight}


def reference(stream, concept_mean, erase_basis, erase_lift, norm_gain, gate_weight, up_weight, down_weight):
    token_rows = stream.reshape(TOKENS, D)
    coords = jnp.dot(token_rows, erase_basis, preferred_element_type=jnp.float32) - jnp.dot(concept_mean, erase_basis, preferred_element_type=jnp.float32)[None, :]
    erased = token_rows.astype(jnp.float32) - jnp.dot(coords, erase_lift.astype(jnp.float32).T, precision=lax.Precision.HIGHEST)
    inv_rms = lax.rsqrt(lax.optimization_barrier(jnp.mean(erased * erased, axis=-1, keepdims=True)) + 1e-05)
    normed = (erased * inv_rms * norm_gain[None, :]).astype(jnp.bfloat16)
    block_width = D // N_SECTION
    normed_blocks = normed.reshape(TOKENS, N_SECTION, block_width).transpose(1, 0, 2)
    gate_blocks = gate_weight.reshape(N_SECTION, block_width, FF)
    up_blocks = up_weight.reshape(N_SECTION, block_width, FF)

    def add_block(totals, pieces):
        rows_block, gate_rows, up_rows = pieces
        gate_part = jnp.dot(rows_block, gate_rows, preferred_element_type=jnp.float32).astype(jnp.bfloat16)
        up_part = jnp.dot(rows_block, up_rows, preferred_element_type=jnp.float32).astype(jnp.bfloat16)
        gate_part, up_part = lax.optimization_barrier((gate_part, up_part))
        return ((totals[0] + gate_part.astype(jnp.float32), totals[1] + up_part.astype(jnp.float32)), None)
    start_sum = (jnp.zeros((TOKENS, FF), jnp.float32), jnp.zeros((TOKENS, FF), jnp.float32))
    (gate, up), _ = lax.scan(add_block, start_sum, (normed_blocks, gate_blocks, up_blocks))
    hidden = (jax.nn.silu(gate) * up).astype(jnp.bfloat16)
    unit_width = FF // N_TENSOR
    hidden_blocks = hidden.reshape(TOKENS, N_TENSOR, unit_width).transpose(1, 0, 2)
    down_blocks = down_weight.reshape(N_TENSOR, unit_width, D)

    def add_down(totals, pieces):
        hidden_block, down_rows = pieces
        term = jnp.dot(hidden_block, down_rows, preferred_element_type=jnp.float32).astype(jnp.bfloat16)
        term = lax.optimization_barrier(term)
        return (totals + term.astype(jnp.float32), None)
    branch, _ = lax.scan(add_down, jnp.zeros((TOKENS, D), jnp.float32), (hidden_blocks, down_blocks))
    return (erased + branch).astype(jnp.bfloat16).reshape(SEQ, MB, D)
```

```python
import jax
import jax.numpy as jnp
from jax import lax
from jax.sharding import PartitionSpec as P


def _stages(n):
    count = n.bit_length() - 1
    assert 1 << count == n
    return count


def _swap(x, axis, n, bit):
    return lax.ppermute(x, axis, perm=[(a, a ^ (1 << bit)) for a in range(n)])


def _all_sum(x, axis, n):
    for bit in range(_stages(n)):
        x = x + _swap(x, axis, n, bit)
    return x


def _pick_chunks(per_t_seq, batch, n_sec):
    for k in (4, 2, 1):
        if per_t_seq % k == 0 and (per_t_seq // k * batch) % n_sec == 0:
            return k
    raise ValueError("no chunking")


def body(
    stream, concept_mean, erase_basis, erase_lift, norm_gain, gate_weight, up_weight, down_weight
):
    seq_rows, batch_count, width_local = stream.shape
    n_sec = lax.axis_size("section")
    n_ten = lax.axis_size("tensor")
    stages = _stages(n_sec)
    sec = lax.axis_index("section")
    ten = lax.axis_index("tensor")
    width = width_local * n_sec
    hidden_local = gate_weight.shape[1]

    local_rows = stream.reshape(seq_rows * batch_count, width_local)
    partial_basis = jnp.dot(local_rows, erase_basis, preferred_element_type=jnp.float32)
    partial_mean = jnp.dot(concept_mean, erase_basis, preferred_element_type=jnp.float32)
    totals = _all_sum(jnp.concatenate([partial_basis, partial_mean[None, :]], axis=0), "section", n_sec)
    coords = totals[:-1] - totals[-1:]
    lift_float = erase_lift.astype(jnp.float32)
    erased = local_rows.astype(jnp.float32) - jnp.dot(
        coords, lift_float.T, precision=lax.Precision.HIGHEST
    )
    squares = _all_sum(jnp.sum(erased * erased, axis=-1), "section", n_sec)
    inv_rms = lax.rsqrt(squares / width + 1e-05)[:, None]
    normed = (erased * inv_rms * norm_gain[None, :]).astype(jnp.bfloat16)

    per_t_seq = seq_rows // n_ten
    chunks = _pick_chunks(per_t_seq, batch_count, n_sec)
    span = per_t_seq // chunks
    part_rows = span * batch_count // n_sec
    order = jnp.bitwise_xor(sec, jnp.arange(n_sec, dtype=sec.dtype))
    grouped = normed.reshape(n_ten, chunks, n_sec, part_rows, width_local)
    grouped = jnp.take(grouped, order, axis=2)
    grouped = grouped.transpose(1, 2, 0, 3, 4)
    block_rows = n_ten * part_rows

    pieces = []
    sent = None
    for k in range(chunks):
        rows_k = grouped[k].reshape(n_sec * block_rows, width_local)
        if sent is not None:
            rows_k, _ = lax.optimization_barrier((rows_k, sent))
        gate_k = jnp.dot(rows_k, gate_weight, preferred_element_type=jnp.float32).astype(jnp.bfloat16)
        up_k = jnp.dot(rows_k, up_weight, preferred_element_type=jnp.float32).astype(jnp.bfloat16)
        cur = jnp.concatenate([gate_k, up_k], axis=-1).reshape(n_sec, block_rows, 2 * hidden_local)
        for bit in range(stages):
            halves = cur.reshape(cur.shape[0] // 2, 2, block_rows, 2 * hidden_local)
            if bit == 0:
                sent = halves[:, 1]
            got = _swap(halves[:, 1], "section", n_sec, bit)
            cur = halves[:, 0].astype(jnp.float32) + got.astype(jnp.float32)
            if bit < stages - 1:
                cur = cur.astype(jnp.bfloat16)
        cur = cur[0]
        hid = (jax.nn.silu(cur[:, :hidden_local]) * cur[:, hidden_local:]).astype(jnp.bfloat16)
        cur = hid[None]
        for bit in reversed(range(stages)):
            got = _swap(cur, "section", n_sec, bit)
            cur = jnp.stack([cur, got], axis=1).reshape(2 * cur.shape[0], block_rows, hidden_local)
        hid_all = cur.reshape(n_sec, n_ten, part_rows, hidden_local).transpose(1, 0, 2, 3)
        hid_all = hid_all.reshape(n_ten * n_sec * part_rows, hidden_local)
        down_k = jnp.dot(hid_all, down_weight, preferred_element_type=jnp.float32).astype(jnp.bfloat16)
        if pieces:
            down_k, _ = lax.optimization_barrier((down_k, pieces[-1]))
        piece = lax.psum_scatter(down_k, "tensor", scatter_dimension=0, tiled=True)
        pieces.append(piece.reshape(n_sec, part_rows, width_local))
    mixed = jnp.take(jnp.stack(pieces), order, axis=1)
    mixed = mixed.reshape(per_t_seq, batch_count, width_local).astype(jnp.float32)
    erased_own = lax.dynamic_slice_in_dim(
        erased.reshape(seq_rows, batch_count, width_local), ten * per_t_seq, per_t_seq, 0
    )
    return (erased_own + mixed).astype(jnp.bfloat16)


def solution(mesh):
    in_specs = (
        P(None, None, "section"),
        P("section"),
        P("section", None),
        P("section", None),
        P("section"),
        P("section", "tensor"),
        P("section", "tensor"),
        P("tensor", "section"),
    )
    out_specs = P("tensor", None, "section")
    return jax.shard_map(body, mesh=mesh, in_specs=in_specs, out_specs=out_specs, check_vma=False)
```

```python
import jax
import jax.numpy as jnp
from jax import lax
from jax.sharding import PartitionSpec as P


_COLS = 2


def _stages(n):
    count = n.bit_length() - 1
    assert 1 << count == n
    return count


def _swap(x, axis, n, bit):
    return lax.ppermute(x, axis, perm=[(a, a ^ (1 << bit)) for a in range(n)])


def _all_sum(x, axis, n):
    for bit in range(_stages(n)):
        x = x + _swap(x, axis, n, bit)
    return x


def _pick_chunks(per_t_seq, batch, n_sec):
    for k in (2, 1):
        if per_t_seq % k == 0 and (per_t_seq // k * batch) % n_sec == 0:
            return k
    raise ValueError("no chunking")


def body(
    stream, concept_mean, erase_basis, erase_lift, norm_gain, gate_weight, up_weight, down_weight
):
    seq_rows, batch_count, width_local = stream.shape
    n_sec = lax.axis_size("section")
    n_ten = lax.axis_size("tensor")
    stages = _stages(n_sec)
    sec = lax.axis_index("section")
    ten = lax.axis_index("tensor")
    width = width_local * n_sec
    hidden_local = gate_weight.shape[1]

    local_rows = stream.reshape(seq_rows * batch_count, width_local)
    partial_basis = jnp.dot(local_rows, erase_basis, preferred_element_type=jnp.float32)
    partial_mean = jnp.dot(concept_mean, erase_basis, preferred_element_type=jnp.float32)
    totals = _all_sum(jnp.concatenate([partial_basis, partial_mean[None, :]], axis=0), "section", n_sec)
    coords = totals[:-1] - totals[-1:]
    lift_float = erase_lift.astype(jnp.float32)
    erased = local_rows.astype(jnp.float32) - jnp.dot(
        coords, lift_float.T, precision=lax.Precision.HIGHEST
    )
    squares = _all_sum(jnp.sum(erased * erased, axis=-1), "section", n_sec)
    inv_rms = lax.rsqrt(squares / width + 1e-05)[:, None]
    normed = (erased * inv_rms * norm_gain[None, :]).astype(jnp.bfloat16)

    per_t_seq = seq_rows // n_ten
    halves_n = _pick_chunks(per_t_seq, batch_count, n_sec)
    span = per_t_seq // halves_n
    part_rows = span * batch_count // n_sec
    order = jnp.bitwise_xor(sec, jnp.arange(n_sec, dtype=sec.dtype))
    grouped = normed.reshape(n_ten, halves_n, n_sec, part_rows, width_local)
    grouped = jnp.take(grouped, order, axis=2)
    grouped = grouped.transpose(1, 2, 0, 3, 4)
    block_rows = n_ten * part_rows
    cols_n = _COLS if hidden_local % (_COLS * 128) == 0 else 1
    cols = hidden_local // cols_n

    pieces = []
    sent = None
    for h in range(halves_n):
        rows_h = grouped[h].reshape(n_sec * block_rows, width_local)
        acc = None
        for c in range(cols_n):
            cut = slice(c * cols, (c + 1) * cols)
            rows_c = rows_h
            if sent is not None:
                rows_c, _ = lax.optimization_barrier((rows_h, sent))
            gate_c = jnp.dot(rows_c, gate_weight[:, cut], preferred_element_type=jnp.float32)
            up_c = jnp.dot(rows_c, up_weight[:, cut], preferred_element_type=jnp.float32)
            cur = jnp.concatenate([gate_c.astype(jnp.bfloat16), up_c.astype(jnp.bfloat16)], axis=-1)
            cur = cur.reshape(n_sec, block_rows, 2 * cols)
            for bit in range(stages):
                halves = cur.reshape(cur.shape[0] // 2, 2, block_rows, 2 * cols)
                if bit == 0:
                    sent = halves[:, 1]
                got = _swap(halves[:, 1], "section", n_sec, bit)
                cur = halves[:, 0].astype(jnp.float32) + got.astype(jnp.float32)
                if bit < stages - 1:
                    cur = cur.astype(jnp.bfloat16)
            cur = cur[0]
            hid = (jax.nn.silu(cur[:, :cols]) * cur[:, cols:]).astype(jnp.bfloat16)
            cur = hid[None]
            for bit in reversed(range(stages)):
                got = _swap(cur, "section", n_sec, bit)
                cur = jnp.stack([cur, got], axis=1).reshape(2 * cur.shape[0], block_rows, cols)
            hid_all = cur.reshape(n_sec, n_ten, part_rows, cols).transpose(1, 0, 2, 3)
            hid_all = hid_all.reshape(n_ten * n_sec * part_rows, cols)
            part = jnp.dot(hid_all, down_weight[cut, :], preferred_element_type=jnp.float32)
            acc = part if acc is None else acc + part
        down_h = acc.astype(jnp.bfloat16)
        piece = lax.psum_scatter(down_h, "tensor", scatter_dimension=0, tiled=True)
        pieces.append(piece.reshape(n_sec, part_rows, width_local))
    mixed = jnp.take(jnp.stack(pieces), order, axis=1)
    mixed = mixed.reshape(per_t_seq, batch_count, width_local).astype(jnp.float32)
    erased_own = lax.dynamic_slice_in_dim(
        erased.reshape(seq_rows, batch_count, width_local), ten * per_t_seq, per_t_seq, 0
    )
    return (erased_own + mixed).astype(jnp.bfloat16)


def solution(mesh):
    in_specs = (
        P(None, None, "section"),
        P("section"),
        P("section", None),
        P("section", None),
        P("section"),
        P("section", "tensor"),
        P("section", "tensor"),
        P("tensor", "section"),
    )
    out_specs = P("tensor", None, "section")
    return jax.shard_map(body, mesh=mesh, in_specs=in_specs, out_specs=out_specs, check_vma=False)
```

```python
import jax
import jax.numpy as jnp
from jax import lax
from jax.sharding import PartitionSpec as P


_COLS = 2


def _stages(n):
    count = n.bit_length() - 1
    assert 1 << count == n
    return count


def _swap(x, axis, n, bit):
    return lax.ppermute(x, axis, perm=[(a, a ^ (1 << bit)) for a in range(n)])


def _all_sum(x, axis, n):
    for bit in range(_stages(n)):
        x = x + _swap(x, axis, n, bit)
    return x


def _scatter_sum(x, axis, n, bit_order):
    count = _stages(n)
    blocks = x.reshape((2,) * count + x.shape[1:])
    for bit in bit_order:
        pos = count - 1 - bit
        pos = pos - sum(1 for done in bit_order[: bit_order.index(bit)] if count - 1 - done < count - 1 - bit)
        keep = lax.index_in_dim(blocks, 0, pos, keepdims=False)
        send = lax.index_in_dim(blocks, 1, pos, keepdims=False)
        got = _swap(send.astype(jnp.bfloat16), axis, n, bit)
        blocks = keep.astype(jnp.float32) + got.astype(jnp.float32)
        if bit != bit_order[-1]:
            blocks = blocks.astype(jnp.bfloat16)
    return blocks


def _pick_chunks(per_t_seq, batch, n_sec):
    for k in (2, 1):
        if per_t_seq % k == 0 and (per_t_seq // k * batch) % n_sec == 0:
            return k
    raise ValueError("no chunking")


def body(
    stream, concept_mean, erase_basis, erase_lift, norm_gain, gate_weight, up_weight, down_weight
):
    seq_rows, batch_count, width_local = stream.shape
    n_sec = lax.axis_size("section")
    n_ten = lax.axis_size("tensor")
    stages = _stages(n_sec)
    sec = lax.axis_index("section")
    ten = lax.axis_index("tensor")
    width = width_local * n_sec
    hidden_local = gate_weight.shape[1]

    local_rows = stream.reshape(seq_rows * batch_count, width_local)
    partial_basis = jnp.dot(local_rows, erase_basis, preferred_element_type=jnp.float32)
    partial_mean = jnp.dot(concept_mean, erase_basis, preferred_element_type=jnp.float32)
    totals = _all_sum(jnp.concatenate([partial_basis, partial_mean[None, :]], axis=0), "section", n_sec)
    coords = totals[:-1] - totals[-1:]
    lift_float = erase_lift.astype(jnp.float32)
    erased = local_rows.astype(jnp.float32) - jnp.dot(
        coords, lift_float.T, precision=lax.Precision.HIGHEST
    )
    squares = _all_sum(jnp.sum(erased * erased, axis=-1), "section", n_sec)
    inv_rms = lax.rsqrt(squares / width + 1e-05)[:, None]
    normed = (erased * inv_rms * norm_gain[None, :]).astype(jnp.bfloat16)

    per_t_seq = seq_rows // n_ten
    halves_n = _pick_chunks(per_t_seq, batch_count, n_sec)
    span = per_t_seq // halves_n
    part_rows = span * batch_count // n_sec
    order = jnp.bitwise_xor(sec, jnp.arange(n_sec, dtype=sec.dtype))
    ten_order = jnp.bitwise_xor(ten, jnp.arange(n_ten, dtype=ten.dtype))
    grouped = normed.reshape(n_ten, halves_n, n_sec, part_rows, width_local)
    grouped = jnp.take(grouped, order, axis=2)
    grouped = grouped.transpose(1, 2, 0, 3, 4)
    block_rows = n_ten * part_rows
    cols_n = _COLS if hidden_local % (_COLS * 128) == 0 else 1
    cols = hidden_local // cols_n

    pieces = []
    sent = None
    for h in range(halves_n):
        rows_h = grouped[h].reshape(n_sec * block_rows, width_local)
        acc = None
        for c in range(cols_n):
            cut = slice(c * cols, (c + 1) * cols)
            rows_c = rows_h
            if sent is not None:
                rows_c, _ = lax.optimization_barrier((rows_h, sent))
            gate_c = jnp.dot(rows_c, gate_weight[:, cut], preferred_element_type=jnp.float32)
            up_c = jnp.dot(rows_c, up_weight[:, cut], preferred_element_type=jnp.float32)
            cur = jnp.concatenate([gate_c.astype(jnp.bfloat16), up_c.astype(jnp.bfloat16)], axis=-1)
            cur = cur.reshape(n_sec, block_rows, 2 * cols)
            for bit in range(stages):
                halves = cur.reshape(cur.shape[0] // 2, 2, block_rows, 2 * cols)
                got = _swap(halves[:, 1], "section", n_sec, bit)
                if bit == 0:
                    sent = got
                cur = halves[:, 0].astype(jnp.float32) + got.astype(jnp.float32)
                if bit < stages - 1:
                    cur = cur.astype(jnp.bfloat16)
            cur = cur[0]
            hid = (jax.nn.silu(cur[:, :cols]) * cur[:, cols:]).astype(jnp.bfloat16)
            cur = hid[None]
            for bit in reversed(range(stages)):
                got = _swap(cur, "section", n_sec, bit)
                cur = jnp.stack([cur, got], axis=1).reshape(2 * cur.shape[0], block_rows, cols)
            hid_all = jnp.take(cur.reshape(n_sec, n_ten, part_rows, cols), ten_order, axis=1)
            hid_all = hid_all.transpose(1, 0, 2, 3)
            hid_all = hid_all.reshape(n_ten * n_sec * part_rows, cols)
            part = jnp.dot(hid_all, down_weight[cut, :], preferred_element_type=jnp.float32)
            acc = part if acc is None else acc + part
        down_h = acc.astype(jnp.bfloat16).reshape(n_ten, n_sec * part_rows, width_local)
        bits = list(range(_stages(n_ten)))
        other = bits[1:2] + bits[:1] + bits[2:]
        half_w = width_local // 2
        piece = jnp.concatenate(
            [
                _scatter_sum(down_h[..., :half_w], "tensor", n_ten, bits),
                _scatter_sum(down_h[..., half_w:], "tensor", n_ten, other),
            ],
            axis=-1,
        )
        pieces.append(piece.reshape(n_sec, part_rows, width_local))
    mixed = jnp.take(jnp.stack(pieces), order, axis=1)
    mixed = mixed.reshape(per_t_seq, batch_count, width_local).astype(jnp.float32)
    erased_own = lax.dynamic_slice_in_dim(
        erased.reshape(seq_rows, batch_count, width_local), ten * per_t_seq, per_t_seq, 0
    )
    return (erased_own + mixed).astype(jnp.bfloat16)


def solution(mesh):
    in_specs = (
        P(None, None, "section"),
        P("section"),
        P("section", None),
        P("section", None),
        P("section"),
        P("section", "tensor"),
        P("section", "tensor"),
        P("tensor", "section"),
    )
    out_specs = P("tensor", None, "section")
    return jax.shard_map(body, mesh=mesh, in_specs=in_specs, out_specs=out_specs, check_vma=False)
```

```python
import jax
import jax.numpy as jnp
from jax import lax
from jax.sharding import PartitionSpec as P


_COLS = 2


def _stages(n):
    count = n.bit_length() - 1
    assert 1 << count == n
    return count


def _swap(x, axis, n, bit):
    return lax.ppermute(x, axis, perm=[(a, a ^ (1 << bit)) for a in range(n)])


def _all_sum(x, axis, n):
    for bit in range(_stages(n)):
        x = x + _swap(x, axis, n, bit)
    return x


def _scatter_sum(x, axis, n, bit_order):
    count = _stages(n)
    blocks = x.reshape((2,) * count + x.shape[1:])
    for bit in bit_order:
        pos = count - 1 - bit
        pos = pos - sum(1 for done in bit_order[: bit_order.index(bit)] if count - 1 - done < count - 1 - bit)
        keep = lax.index_in_dim(blocks, 0, pos, keepdims=False)
        send = lax.index_in_dim(blocks, 1, pos, keepdims=False)
        got = _swap(send.astype(jnp.bfloat16), axis, n, bit)
        blocks = keep.astype(jnp.float32) + got.astype(jnp.float32)
        if bit != bit_order[-1]:
            blocks = blocks.astype(jnp.bfloat16)
    return blocks


def _pick_chunks(per_t_seq, batch, n_sec):
    for k in (2, 1):
        if per_t_seq % k == 0 and (per_t_seq // k * batch) % n_sec == 0:
            return k
    raise ValueError("no chunking")


def body(
    stream, concept_mean, erase_basis, erase_lift, norm_gain, gate_weight, up_weight, down_weight
):
    seq_rows, batch_count, width_local = stream.shape
    n_sec = lax.axis_size("section")
    n_ten = lax.axis_size("tensor")
    stages = _stages(n_sec)
    sec = lax.axis_index("section")
    ten = lax.axis_index("tensor")
    width = width_local * n_sec
    hidden_local = gate_weight.shape[1]

    local_rows = stream.reshape(seq_rows * batch_count, width_local)
    partial_basis = jnp.dot(local_rows, erase_basis, preferred_element_type=jnp.float32)
    partial_mean = jnp.dot(concept_mean, erase_basis, preferred_element_type=jnp.float32)
    totals = _all_sum(jnp.concatenate([partial_basis, partial_mean[None, :]], axis=0), "section", n_sec)
    coords = totals[:-1] - totals[-1:]
    lift_float = erase_lift.astype(jnp.float32)
    erased = local_rows.astype(jnp.float32) - jnp.dot(
        coords, lift_float.T, precision=lax.Precision.HIGHEST
    )
    squares = _all_sum(jnp.sum(erased * erased, axis=-1), "section", n_sec)
    inv_rms = lax.rsqrt(squares / width + 1e-05)[:, None]
    normed = (erased * inv_rms * norm_gain[None, :]).astype(jnp.bfloat16)

    per_t_seq = seq_rows // n_ten
    halves_n = _pick_chunks(per_t_seq, batch_count, n_sec)
    span = per_t_seq // halves_n
    part_rows = span * batch_count // n_sec
    order = jnp.bitwise_xor(sec, jnp.arange(n_sec, dtype=sec.dtype))
    ten_order = jnp.bitwise_xor(ten, jnp.arange(n_ten, dtype=ten.dtype))
    grouped = normed.reshape(n_ten, halves_n, n_sec, part_rows, width_local)
    grouped = jnp.take(grouped, order, axis=2)
    grouped = grouped.transpose(1, 2, 0, 3, 4)
    block_rows = n_ten * part_rows
    cols_n = _COLS if hidden_local % (_COLS * 128) == 0 else 1
    cols = hidden_local // cols_n

    pieces = []
    sent = None
    for h in range(halves_n):
        rows_h = grouped[h].reshape(n_sec * block_rows, width_local)
        hid_parts = []
        for c in range(cols_n):
            cut = slice(c * cols, (c + 1) * cols)
            rows_c = rows_h
            if sent is not None:
                rows_c, _ = lax.optimization_barrier((rows_h, sent))
            if h > 0 and c == cols_n - 1:
                rows_c, _ = lax.optimization_barrier((rows_c, down_h))
            gate_c = jnp.dot(rows_c, gate_weight[:, cut], preferred_element_type=jnp.float32)
            up_c = jnp.dot(rows_c, up_weight[:, cut], preferred_element_type=jnp.float32)
            cur = jnp.concatenate([gate_c.astype(jnp.bfloat16), up_c.astype(jnp.bfloat16)], axis=-1)
            cur = cur.reshape(n_sec, block_rows, 2 * cols)
            for bit in range(stages):
                halves = cur.reshape(cur.shape[0] // 2, 2, block_rows, 2 * cols)
                got = _swap(halves[:, 1], "section", n_sec, bit)
                if bit == 0:
                    sent = got
                cur = halves[:, 0].astype(jnp.float32) + got.astype(jnp.float32)
                if bit < stages - 1:
                    cur = cur.astype(jnp.bfloat16)
            cur = cur[0]
            hid = (jax.nn.silu(cur[:, :cols]) * cur[:, cols:]).astype(jnp.bfloat16)
            cur = hid[None]
            for bit in reversed(range(stages)):
                got = _swap(cur, "section", n_sec, bit)
                cur = jnp.stack([cur, got], axis=1).reshape(2 * cur.shape[0], block_rows, cols)
            hid_parts.append(cur.reshape(n_sec, n_ten, part_rows, cols))
        hid_all = jnp.take(jnp.concatenate(hid_parts, axis=-1), ten_order, axis=1)
        hid_all = hid_all.transpose(1, 0, 2, 3).reshape(n_ten * n_sec * part_rows, hidden_local)
        acc = jnp.dot(hid_all, down_weight, preferred_element_type=jnp.float32)
        down_h = acc.astype(jnp.bfloat16).reshape(n_ten, n_sec * part_rows, width_local)
        bits = list(range(_stages(n_ten)))
        other = bits[1:2] + bits[:1] + bits[2:]
        half_w = width_local // 2
        piece = jnp.concatenate(
            [
                _scatter_sum(down_h[..., :half_w], "tensor", n_ten, bits),
                _scatter_sum(down_h[..., half_w:], "tensor", n_ten, other),
            ],
            axis=-1,
        )
        pieces.append(piece.reshape(n_sec, part_rows, width_local))
    mixed = jnp.take(jnp.stack(pieces), order, axis=1)
    mixed = mixed.reshape(per_t_seq, batch_count, width_local).astype(jnp.float32)
    own_rows = per_t_seq * batch_count
    erased_own = lax.dynamic_slice_in_dim(erased, ten * own_rows, own_rows, 0)
    erased_own = erased_own.reshape(per_t_seq, batch_count, width_local)
    return (erased_own + mixed).astype(jnp.bfloat16)


def solution(mesh):
    in_specs = (
        P(None, None, "section"),
        P("section"),
        P("section", None),
        P("section", None),
        P("section"),
        P("section", "tensor"),
        P("section", "tensor"),
        P("tensor", "section"),
    )
    out_specs = P("tensor", None, "section")
    return jax.shard_map(body, mesh=mesh, in_specs=in_specs, out_specs=out_specs, check_vma=False)
```

```python
import jax
import jax.numpy as jnp
from jax import lax
from jax.sharding import PartitionSpec as P


_COLS = 2


def _stages(n):
    count = n.bit_length() - 1
    assert 1 << count == n
    return count


def _swap(x, axis, n, bit):
    return lax.ppermute(x, axis, perm=[(a, a ^ (1 << bit)) for a in range(n)])


def _all_sum(x, axis, n):
    for bit in range(_stages(n)):
        x = x + _swap(x, axis, n, bit)
    return x


def _scatter_sum(x, axis, n, bit_order):
    count = _stages(n)
    blocks = x.reshape((2,) * count + x.shape[1:])
    for bit in bit_order:
        pos = count - 1 - bit
        pos = pos - sum(1 for done in bit_order[: bit_order.index(bit)] if count - 1 - done < count - 1 - bit)
        keep = lax.index_in_dim(blocks, 0, pos, keepdims=False)
        send = lax.index_in_dim(blocks, 1, pos, keepdims=False)
        got = _swap(send.astype(jnp.bfloat16), axis, n, bit)
        blocks = keep.astype(jnp.float32) + got.astype(jnp.float32)
        if bit != bit_order[-1]:
            blocks = blocks.astype(jnp.bfloat16)
    return blocks


def _pick_chunks(per_t_seq, batch, n_sec):
    for k in (2, 1):
        if per_t_seq % k == 0 and (per_t_seq // k * batch) % n_sec == 0:
            return k
    raise ValueError("no chunking")


def body(
    stream, concept_mean, erase_basis, erase_lift, norm_gain, gate_weight, up_weight, down_weight
):
    seq_rows, batch_count, width_local = stream.shape
    n_sec = lax.axis_size("section")
    n_ten = lax.axis_size("tensor")
    stages = _stages(n_sec)
    sec = lax.axis_index("section")
    ten = lax.axis_index("tensor")
    width = width_local * n_sec
    hidden_local = gate_weight.shape[1]

    local_rows = stream.reshape(seq_rows * batch_count, width_local)
    partial_basis = jnp.dot(local_rows, erase_basis, preferred_element_type=jnp.float32)
    partial_mean = jnp.dot(concept_mean, erase_basis, preferred_element_type=jnp.float32)
    totals = _all_sum(jnp.concatenate([partial_basis, partial_mean[None, :]], axis=0), "section", n_sec)
    coords = totals[:-1] - totals[-1:]
    lift_float = erase_lift.astype(jnp.float32)
    erased = local_rows.astype(jnp.float32) - jnp.dot(
        coords, lift_float.T, precision=lax.Precision.HIGHEST
    )
    squares = _all_sum(jnp.sum(erased * erased, axis=-1), "section", n_sec)
    inv_rms = lax.rsqrt(squares / width + 1e-05)[:, None]
    normed = (erased * inv_rms * norm_gain[None, :]).astype(jnp.bfloat16)

    per_t_seq = seq_rows // n_ten
    halves_n = _pick_chunks(per_t_seq, batch_count, n_sec)
    span = per_t_seq // halves_n
    part_rows = span * batch_count // n_sec
    order = jnp.bitwise_xor(sec, jnp.arange(n_sec, dtype=sec.dtype))
    ten_order = jnp.bitwise_xor(ten, jnp.arange(n_ten, dtype=ten.dtype))
    grouped = normed.reshape(n_ten, halves_n, n_sec, part_rows, width_local)
    grouped = jnp.take(grouped, order, axis=2)
    grouped = grouped.transpose(1, 2, 0, 3, 4)
    block_rows = n_ten * part_rows
    cols_n = _COLS if hidden_local % (_COLS * 128) == 0 else 1
    cols = hidden_local // cols_n

    def front(rows, cut):
        gate_c = jnp.dot(rows, gate_weight[:, cut], preferred_element_type=jnp.float32)
        up_c = jnp.dot(rows, up_weight[:, cut], preferred_element_type=jnp.float32)
        cur = jnp.concatenate([gate_c.astype(jnp.bfloat16), up_c.astype(jnp.bfloat16)], axis=-1)
        made = cur
        cur = cur.reshape(n_sec, block_rows, 2 * cols)
        first = None
        for bit in range(stages):
            halves = cur.reshape(cur.shape[0] // 2, 2, block_rows, 2 * cols)
            got = _swap(halves[:, 1], "section", n_sec, bit)
            if bit == 0:
                first = got
            cur = halves[:, 0].astype(jnp.float32) + got.astype(jnp.float32)
            if bit < stages - 1:
                cur = cur.astype(jnp.bfloat16)
        return cur[0], made, first

    def back(cur):
        hid = (jax.nn.silu(cur[:, :cols]) * cur[:, cols:]).astype(jnp.bfloat16)
        cur = hid[None]
        for bit in reversed(range(stages)):
            got = _swap(cur, "section", n_sec, bit)
            cur = jnp.stack([cur, got], axis=1).reshape(2 * cur.shape[0], block_rows, cols)
        return cur.reshape(n_sec, n_ten, part_rows, cols)

    def finish(hid_parts):
        hid_all = jnp.take(jnp.concatenate(hid_parts, axis=-1), ten_order, axis=1)
        hid_all = hid_all.transpose(1, 0, 2, 3).reshape(n_ten * n_sec * part_rows, hidden_local)
        acc = jnp.dot(hid_all, down_weight, preferred_element_type=jnp.float32)
        return acc.astype(jnp.bfloat16).reshape(n_ten, n_sec * part_rows, width_local)

    def scatter(down_h):
        bits = list(range(_stages(n_ten)))
        other = bits[1:2] + bits[:1] + bits[2:]
        half_w = width_local // 2
        piece = jnp.concatenate(
            [
                _scatter_sum(down_h[..., :half_w], "tensor", n_ten, bits),
                _scatter_sum(down_h[..., half_w:], "tensor", n_ten, other),
            ],
            axis=-1,
        )
        return piece.reshape(n_sec, part_rows, width_local)

    plan = [(h, c) for h in range(halves_n) for c in range(cols_n)]
    hid_parts = [[] for _ in range(halves_n)]
    downs = [None] * halves_n
    pending = None
    sent = None
    for h, c in plan:
        rows = grouped[h].reshape(n_sec * block_rows, width_local)
        if sent is not None:
            rows, _ = lax.optimization_barrier((rows, sent))
        if h > 0 and c == cols_n - 1 and downs[h - 1] is not None:
            rows, _ = lax.optimization_barrier((rows, downs[h - 1]))
        reduced, made, sent = front(rows, slice(c * cols, (c + 1) * cols))
        if pending is not None:
            prev_h, prev = pending
            prev, _ = lax.optimization_barrier((prev, made))
            hid_parts[prev_h].append(back(prev))
            if len(hid_parts[prev_h]) == cols_n:
                downs[prev_h] = finish(hid_parts[prev_h])
        pending = (h, reduced)
    prev_h, prev = pending
    hid_parts[prev_h].append(back(prev))
    downs[prev_h] = finish(hid_parts[prev_h])
    pieces = [scatter(down_h) for down_h in downs]
    mixed = jnp.take(jnp.stack(pieces), order, axis=1)
    mixed = mixed.reshape(per_t_seq, batch_count, width_local).astype(jnp.float32)
    own_rows = per_t_seq * batch_count
    erased_own = lax.dynamic_slice_in_dim(erased, ten * own_rows, own_rows, 0)
    erased_own = erased_own.reshape(per_t_seq, batch_count, width_local)
    return (erased_own + mixed).astype(jnp.bfloat16)


def solution(mesh):
    in_specs = (
        P(None, None, "section"),
        P("section"),
        P("section", None),
        P("section", None),
        P("section"),
        P("section", "tensor"),
        P("section", "tensor"),
        P("tensor", "section"),
    )
    out_specs = P("tensor", None, "section")
    return jax.shard_map(body, mesh=mesh, in_specs=in_specs, out_specs=out_specs, check_vma=False)
```

```python
import jax
import jax.numpy as jnp
from jax import lax
from jax.sharding import PartitionSpec as P


_COLS = 2


def _stages(n):
    count = n.bit_length() - 1
    assert 1 << count == n
    return count


def _swap(x, axis, n, bit):
    return lax.ppermute(x, axis, perm=[(a, a ^ (1 << bit)) for a in range(n)])


def _all_sum(x, axis, n):
    for bit in range(_stages(n)):
        x = x + _swap(x, axis, n, bit)
    return x


def _scatter_sum(x, axis, n, bit_order):
    count = _stages(n)
    blocks = x.reshape((2,) * count + x.shape[1:])
    for bit in bit_order:
        pos = count - 1 - bit
        pos = pos - sum(1 for done in bit_order[: bit_order.index(bit)] if count - 1 - done < count - 1 - bit)
        keep = lax.index_in_dim(blocks, 0, pos, keepdims=False)
        send = lax.index_in_dim(blocks, 1, pos, keepdims=False)
        got = _swap(send.astype(jnp.bfloat16), axis, n, bit)
        blocks = keep.astype(jnp.float32) + got.astype(jnp.float32)
        if bit != bit_order[-1]:
            blocks = blocks.astype(jnp.bfloat16)
    return blocks


def _pick_chunks(per_t_seq, batch, n_sec):
    for k in (2, 1):
        if per_t_seq % k == 0 and (per_t_seq // k * batch) % n_sec == 0:
            return k
    raise ValueError("no chunking")


def body(
    stream, concept_mean, erase_basis, erase_lift, norm_gain, gate_weight, up_weight, down_weight
):
    seq_rows, batch_count, width_local = stream.shape
    n_sec = lax.axis_size("section")
    n_ten = lax.axis_size("tensor")
    stages = _stages(n_sec)
    sec = lax.axis_index("section")
    ten = lax.axis_index("tensor")
    width = width_local * n_sec
    hidden_local = gate_weight.shape[1]

    local_rows = stream.reshape(seq_rows * batch_count, width_local)
    partial_basis = jnp.dot(local_rows, erase_basis, preferred_element_type=jnp.float32)
    partial_mean = jnp.dot(concept_mean, erase_basis, preferred_element_type=jnp.float32)
    totals = _all_sum(jnp.concatenate([partial_basis, partial_mean[None, :]], axis=0), "section", n_sec)
    coords = totals[:-1] - totals[-1:]
    lift_float = erase_lift.astype(jnp.float32)
    erased = local_rows.astype(jnp.float32) - jnp.dot(
        coords, lift_float.T, precision=lax.Precision.HIGHEST
    )
    squares = _all_sum(jnp.sum(erased * erased, axis=-1), "section", n_sec)
    inv_rms = lax.rsqrt(squares / width + 1e-05)[:, None]
    normed = (erased * inv_rms * norm_gain[None, :]).astype(jnp.bfloat16)

    per_t_seq = seq_rows // n_ten
    halves_n = _pick_chunks(per_t_seq, batch_count, n_sec)
    span = per_t_seq // halves_n
    part_rows = span * batch_count // n_sec
    order = jnp.bitwise_xor(sec, jnp.arange(n_sec, dtype=sec.dtype))
    ten_order = jnp.bitwise_xor(ten, jnp.arange(n_ten, dtype=ten.dtype))
    grouped = normed.reshape(n_ten, halves_n, n_sec, part_rows, width_local)
    grouped = jnp.take(grouped, order, axis=2)
    grouped = grouped.transpose(1, 2, 0, 3, 4)
    block_rows = n_ten * part_rows
    cols_n = _COLS if hidden_local % (_COLS * 128) == 0 else 1
    cols = hidden_local // cols_n

    def front(rows, cut):
        gate_c = jnp.dot(rows, gate_weight[:, cut], preferred_element_type=jnp.float32)
        up_c = jnp.dot(rows, up_weight[:, cut], preferred_element_type=jnp.float32)
        cur = jnp.concatenate([gate_c.astype(jnp.bfloat16), up_c.astype(jnp.bfloat16)], axis=-1)
        made = cur
        cur = cur.reshape(n_sec, block_rows, 2 * cols)
        first = None
        for bit in range(stages):
            halves = cur.reshape(cur.shape[0] // 2, 2, block_rows, 2 * cols)
            if bit == stages - 1:
                first = halves[:, 1]
            got = _swap(halves[:, 1], "section", n_sec, bit)
            cur = halves[:, 0].astype(jnp.float32) + got.astype(jnp.float32)
            if bit < stages - 1:
                cur = cur.astype(jnp.bfloat16)
        return cur[0], made, first

    def back(cur):
        hid = (jax.nn.silu(cur[:, :cols]) * cur[:, cols:]).astype(jnp.bfloat16)
        cur = hid[None]
        for bit in reversed(range(stages)):
            got = _swap(cur, "section", n_sec, bit)
            cur = jnp.stack([cur, got], axis=1).reshape(2 * cur.shape[0], block_rows, cols)
        return cur.reshape(n_sec, n_ten, part_rows, cols)

    def finish(hid_parts):
        hid_all = jnp.take(jnp.concatenate(hid_parts, axis=-1), ten_order, axis=1)
        hid_all = hid_all.transpose(1, 0, 2, 3).reshape(n_ten * n_sec * part_rows, hidden_local)
        acc = jnp.dot(hid_all, down_weight, preferred_element_type=jnp.float32)
        return acc.astype(jnp.bfloat16).reshape(n_ten, n_sec * part_rows, width_local)

    def scatter(down_h):
        bits = list(range(_stages(n_ten)))
        other = bits[1:2] + bits[:1] + bits[2:]
        half_w = width_local // 2
        piece = jnp.concatenate(
            [
                _scatter_sum(down_h[..., :half_w], "tensor", n_ten, bits),
                _scatter_sum(down_h[..., half_w:], "tensor", n_ten, other),
            ],
            axis=-1,
        )
        return piece.reshape(n_sec, part_rows, width_local)

    plan = [(h, c) for h in range(halves_n) for c in range(cols_n)]
    hid_parts = [[] for _ in range(halves_n)]
    downs = [None] * halves_n
    pending = None
    sent = None
    for h, c in plan:
        rows = grouped[h].reshape(n_sec * block_rows, width_local)
        if sent is not None:
            rows, _ = lax.optimization_barrier((rows, sent))
        if h > 0 and c == cols_n - 1 and downs[h - 1] is not None:
            rows, _ = lax.optimization_barrier((rows, downs[h - 1]))
        reduced, made, sent = front(rows, slice(c * cols, (c + 1) * cols))
        if pending is not None:
            prev_h, prev = pending
            prev, _ = lax.optimization_barrier((prev, made))
            hid_parts[prev_h].append(back(prev))
            if len(hid_parts[prev_h]) == cols_n:
                downs[prev_h] = finish(hid_parts[prev_h])
        pending = (h, reduced)
    prev_h, prev = pending
    hid_parts[prev_h].append(back(prev))
    downs[prev_h] = finish(hid_parts[prev_h])
    pieces = [scatter(down_h) for down_h in downs]
    mixed = jnp.take(jnp.stack(pieces), order, axis=1)
    mixed = mixed.reshape(per_t_seq, batch_count, width_local).astype(jnp.float32)
    own_rows = per_t_seq * batch_count
    erased_own = lax.dynamic_slice_in_dim(erased, ten * own_rows, own_rows, 0)
    erased_own = erased_own.reshape(per_t_seq, batch_count, width_local)
    return (erased_own + mixed).astype(jnp.bfloat16)


def solution(mesh):
    in_specs = (
        P(None, None, "section"),
        P("section"),
        P("section", None),
        P("section", None),
        P("section"),
        P("section", "tensor"),
        P("section", "tensor"),
        P("tensor", "section"),
    )
    out_specs = P("tensor", None, "section")
    return jax.shard_map(body, mesh=mesh, in_specs=in_specs, out_specs=out_specs, check_vma=False)
```

```python
import jax
import jax.numpy as jnp
from jax import lax
from jax.sharding import PartitionSpec as P


_COLS = 2


def _stages(n):
    count = n.bit_length() - 1
    assert 1 << count == n
    return count


def _swap(x, axis, n, bit):
    return lax.ppermute(x, axis, perm=[(a, a ^ (1 << bit)) for a in range(n)])


def _all_sum(x, axis, n):
    for bit in range(_stages(n)):
        x = x + _swap(x, axis, n, bit)
    return x


def _scatter_sum(x, axis, n, bit_order):
    count = _stages(n)
    blocks = x.reshape((2,) * count + x.shape[1:])
    for bit in bit_order:
        pos = count - 1 - bit
        pos = pos - sum(1 for done in bit_order[: bit_order.index(bit)] if count - 1 - done < count - 1 - bit)
        keep = lax.index_in_dim(blocks, 0, pos, keepdims=False)
        send = lax.index_in_dim(blocks, 1, pos, keepdims=False)
        got = _swap(send.astype(jnp.bfloat16), axis, n, bit)
        blocks = keep.astype(jnp.float32) + got.astype(jnp.float32)
        if bit != bit_order[-1]:
            blocks = blocks.astype(jnp.bfloat16)
    return blocks


def _pick_chunks(per_t_seq, batch, n_sec):
    for k in (2, 1):
        if per_t_seq % k == 0 and (per_t_seq // k * batch) % n_sec == 0:
            return k
    raise ValueError("no chunking")


def body(
    stream, concept_mean, erase_basis, erase_lift, norm_gain, gate_weight, up_weight, down_weight
):
    seq_rows, batch_count, width_local = stream.shape
    n_sec = lax.axis_size("section")
    n_ten = lax.axis_size("tensor")
    stages = _stages(n_sec)
    sec = lax.axis_index("section")
    ten = lax.axis_index("tensor")
    width = width_local * n_sec
    hidden_local = gate_weight.shape[1]

    local_rows = stream.reshape(seq_rows * batch_count, width_local)
    partial_basis = jnp.dot(local_rows, erase_basis, preferred_element_type=jnp.float32)
    partial_mean = jnp.dot(concept_mean, erase_basis, preferred_element_type=jnp.float32)
    totals = _all_sum(jnp.concatenate([partial_basis, partial_mean[None, :]], axis=0), "section", n_sec)
    coords = totals[:-1] - totals[-1:]
    lift_float = erase_lift.astype(jnp.float32)
    erased = local_rows.astype(jnp.float32) - jnp.dot(
        coords, lift_float.T, precision=lax.Precision.HIGHEST
    )
    squares = _all_sum(jnp.sum(erased * erased, axis=-1), "section", n_sec)
    inv_rms = lax.rsqrt(squares / width + 1e-05)[:, None]
    normed = (erased * inv_rms * norm_gain[None, :]).astype(jnp.bfloat16)

    per_t_seq = seq_rows // n_ten
    halves_n = _pick_chunks(per_t_seq, batch_count, n_sec)
    span = per_t_seq // halves_n
    part_rows = span * batch_count // n_sec
    order = jnp.bitwise_xor(sec, jnp.arange(n_sec, dtype=sec.dtype))
    ten_order = jnp.bitwise_xor(ten, jnp.arange(n_ten, dtype=ten.dtype))
    grouped = normed.reshape(n_ten, halves_n, n_sec, part_rows, width_local)
    grouped = jnp.take(grouped, order, axis=2)
    grouped = grouped.transpose(1, 2, 0, 3, 4)
    block_rows = n_ten * part_rows
    cols_n = _COLS if hidden_local % (_COLS * 128) == 0 else 1
    cols = hidden_local // cols_n

    def front(rows, cut):
        gate_c = jnp.dot(rows, gate_weight[:, cut], preferred_element_type=jnp.float32)
        up_c = jnp.dot(rows, up_weight[:, cut], preferred_element_type=jnp.float32)
        cur = jnp.concatenate([gate_c.astype(jnp.bfloat16), up_c.astype(jnp.bfloat16)], axis=-1)
        made = cur
        cur = cur.reshape(n_sec, block_rows, 2 * cols)
        first = None
        for bit in range(stages):
            halves = cur.reshape(cur.shape[0] // 2, 2, block_rows, 2 * cols)
            if bit == stages - 1:
                first = halves[:, 1]
            got = _swap(halves[:, 1], "section", n_sec, bit)
            cur = halves[:, 0].astype(jnp.float32) + got.astype(jnp.float32)
            if bit < stages - 1:
                cur = cur.astype(jnp.bfloat16)
        return cur[0], made, first

    def back_a(cur):
        hid = (jax.nn.silu(cur[:, :cols]) * cur[:, cols:]).astype(jnp.bfloat16)
        cur = hid[None]
        return cur, _swap(cur, "section", n_sec, stages - 1)

    def back_b(cur, got):
        cur = jnp.stack([cur, got], axis=1).reshape(2 * cur.shape[0], block_rows, cols)
        for bit in reversed(range(stages - 1)):
            got = _swap(cur, "section", n_sec, bit)
            cur = jnp.stack([cur, got], axis=1).reshape(2 * cur.shape[0], block_rows, cols)
        return cur.reshape(n_sec, n_ten, part_rows, cols)

    def finish(hid_parts):
        hid_all = jnp.take(jnp.concatenate(hid_parts, axis=-1), ten_order, axis=1)
        hid_all = hid_all.transpose(1, 0, 2, 3).reshape(n_ten * n_sec * part_rows, hidden_local)
        acc = jnp.dot(hid_all, down_weight, preferred_element_type=jnp.float32)
        return acc.astype(jnp.bfloat16).reshape(n_ten, n_sec * part_rows, width_local)

    def scatter(down_h):
        bits = list(range(_stages(n_ten)))
        other = bits[1:2] + bits[:1] + bits[2:]
        half_w = width_local // 2
        piece = jnp.concatenate(
            [
                _scatter_sum(down_h[..., :half_w], "tensor", n_ten, bits),
                _scatter_sum(down_h[..., half_w:], "tensor", n_ten, other),
            ],
            axis=-1,
        )
        return piece.reshape(n_sec, part_rows, width_local)

    plan = [(h, c) for h in range(halves_n) for c in range(cols_n)]
    hid_parts = [[] for _ in range(halves_n)]
    downs = [None] * halves_n
    pending = None
    waiting = []
    sent = None

    def land(made):
        prev_h, cur, got = waiting.pop(0)
        if made is not None:
            got, _ = lax.optimization_barrier((got, made))
        hid_parts[prev_h].append(back_b(cur, got))
        if len(hid_parts[prev_h]) == cols_n:
            downs[prev_h] = finish(hid_parts[prev_h])

    for h, c in plan:
        rows = grouped[h].reshape(n_sec * block_rows, width_local)
        if sent is not None:
            rows, _ = lax.optimization_barrier((rows, sent))
        if h > 0 and c == cols_n - 1 and downs[h - 1] is not None:
            rows, _ = lax.optimization_barrier((rows, downs[h - 1]))
        reduced, made, sent = front(rows, slice(c * cols, (c + 1) * cols))
        if len(waiting) == 1:
            land(made)
        if pending is not None:
            prev_h, prev = pending
            prev, _ = lax.optimization_barrier((prev, made))
            waiting.append((prev_h,) + back_a(prev))
        pending = (h, reduced)
    prev_h, prev = pending
    waiting.append((prev_h,) + back_a(prev))
    while waiting:
        land(None)
    pieces = [scatter(down_h) for down_h in downs]
    mixed = jnp.take(jnp.stack(pieces), order, axis=1)
    mixed = mixed.reshape(per_t_seq, batch_count, width_local).astype(jnp.float32)
    own_rows = per_t_seq * batch_count
    erased_own = lax.dynamic_slice_in_dim(erased, ten * own_rows, own_rows, 0)
    erased_own = erased_own.reshape(per_t_seq, batch_count, width_local)
    return (erased_own + mixed).astype(jnp.bfloat16)


def solution(mesh):
    in_specs = (
        P(None, None, "section"),
        P("section"),
        P("section", None),
        P("section", None),
        P("section"),
        P("section", "tensor"),
        P("section", "tensor"),
        P("tensor", "section"),
    )
    out_specs = P("tensor", None, "section")
    return jax.shard_map(body, mesh=mesh, in_specs=in_specs, out_specs=out_specs, check_vma=False)
```

```python
import jax
import jax.numpy as jnp
from jax import lax
from jax.sharding import PartitionSpec as P


_COLS = 2


def _stages(n):
    count = n.bit_length() - 1
    assert 1 << count == n
    return count


def _swap(x, axis, n, bit):
    return lax.ppermute(x, axis, perm=[(a, a ^ (1 << bit)) for a in range(n)])


def _all_sum(x, axis, n):
    for bit in range(_stages(n)):
        x = x + _swap(x, axis, n, bit)
    return x


def _scatter_sum(x, axis, n, bit_order):
    count = _stages(n)
    blocks = x.reshape((2,) * count + x.shape[1:])
    for bit in bit_order:
        pos = count - 1 - bit
        pos = pos - sum(1 for done in bit_order[: bit_order.index(bit)] if count - 1 - done < count - 1 - bit)
        keep = lax.index_in_dim(blocks, 0, pos, keepdims=False)
        send = lax.index_in_dim(blocks, 1, pos, keepdims=False)
        got = _swap(send.astype(jnp.bfloat16), axis, n, bit)
        blocks = keep.astype(jnp.float32) + got.astype(jnp.float32)
        if bit != bit_order[-1]:
            blocks = blocks.astype(jnp.bfloat16)
    return blocks


def _pick_chunks(per_t_seq, batch, n_sec):
    for k in (2, 1):
        if per_t_seq % k == 0 and (per_t_seq // k * batch) % n_sec == 0:
            return k
    raise ValueError("no chunking")


def body(
    stream, concept_mean, erase_basis, erase_lift, norm_gain, gate_weight, up_weight, down_weight
):
    seq_rows, batch_count, width_local = stream.shape
    n_sec = lax.axis_size("section")
    n_ten = lax.axis_size("tensor")
    stages = _stages(n_sec)
    sec = lax.axis_index("section")
    ten = lax.axis_index("tensor")
    width = width_local * n_sec
    hidden_local = gate_weight.shape[1]

    local_rows = stream.reshape(seq_rows * batch_count, width_local)
    partial_basis = jnp.dot(local_rows, erase_basis, preferred_element_type=jnp.float32)
    partial_mean = jnp.dot(concept_mean, erase_basis, preferred_element_type=jnp.float32)
    totals = _all_sum(jnp.concatenate([partial_basis, partial_mean[None, :]], axis=0), "section", n_sec)
    coords = totals[:-1] - totals[-1:]
    lift_float = erase_lift.astype(jnp.float32)
    erased = local_rows.astype(jnp.float32) - jnp.dot(
        coords, lift_float.T, precision=lax.Precision.HIGHEST
    )
    squares = _all_sum(jnp.sum(erased * erased, axis=-1), "section", n_sec)
    inv_rms = lax.rsqrt(squares / width + 1e-05)[:, None]
    normed = (erased * inv_rms * norm_gain[None, :]).astype(jnp.bfloat16)

    per_t_seq = seq_rows // n_ten
    halves_n = _pick_chunks(per_t_seq, batch_count, n_sec)
    span = per_t_seq // halves_n
    part_rows = span * batch_count // n_sec
    order = jnp.bitwise_xor(sec, jnp.arange(n_sec, dtype=sec.dtype))
    ten_order = jnp.bitwise_xor(ten, jnp.arange(n_ten, dtype=ten.dtype))
    grouped = normed.reshape(n_ten, halves_n, n_sec, part_rows, width_local)
    grouped = jnp.take(grouped, order, axis=2)
    grouped = grouped.transpose(1, 2, 0, 3, 4)
    block_rows = n_ten * part_rows
    cols_n = _COLS if hidden_local % (_COLS * 128) == 0 else 1
    cols = hidden_local // cols_n

    def front(rows, cut):
        gate_c = jnp.dot(rows, gate_weight[:, cut], preferred_element_type=jnp.float32)
        up_c = jnp.dot(rows, up_weight[:, cut], preferred_element_type=jnp.float32)
        cur = jnp.concatenate([gate_c.astype(jnp.bfloat16), up_c.astype(jnp.bfloat16)], axis=-1)
        made = cur
        cur = cur.reshape(n_sec, block_rows, 2 * cols)
        first = None
        for bit in range(stages):
            halves = cur.reshape(cur.shape[0] // 2, 2, block_rows, 2 * cols)
            if bit == stages - 1:
                first = halves[:, 1]
            got = _swap(halves[:, 1], "section", n_sec, bit)
            cur = halves[:, 0].astype(jnp.float32) + got.astype(jnp.float32)
            if bit < stages - 1:
                cur = cur.astype(jnp.bfloat16)
        return cur[0], made, first

    def back_a(cur):
        hid = (jax.nn.silu(cur[:, :cols]) * cur[:, cols:]).astype(jnp.bfloat16)
        cur = hid[None]
        return cur, _swap(cur, "section", n_sec, stages - 1)

    def back_b(cur, got):
        cur = jnp.stack([cur, got], axis=1).reshape(2 * cur.shape[0], block_rows, cols)
        for bit in reversed(range(stages - 1)):
            got = _swap(cur, "section", n_sec, bit)
            cur = jnp.stack([cur, got], axis=1).reshape(2 * cur.shape[0], block_rows, cols)
        return cur.reshape(n_sec, n_ten, part_rows, cols)

    def finish(hid_parts):
        hid_all = jnp.take(jnp.concatenate(hid_parts, axis=-1), ten_order, axis=1)
        hid_all = hid_all.transpose(1, 0, 2, 3).reshape(n_ten * n_sec * part_rows, hidden_local)
        acc = jnp.dot(hid_all, down_weight, preferred_element_type=jnp.float32)
        return acc.astype(jnp.bfloat16).reshape(n_ten, n_sec * part_rows, width_local)

    def scatter(down_h):
        bits = list(range(_stages(n_ten)))
        other = bits[1:2] + bits[:1] + bits[2:]
        half_w = width_local // 2
        piece = jnp.concatenate(
            [
                _scatter_sum(down_h[..., :half_w], "tensor", n_ten, bits),
                _scatter_sum(down_h[..., half_w:], "tensor", n_ten, other),
            ],
            axis=-1,
        )
        return piece.reshape(n_sec, part_rows, width_local)

    plan = [(h, c) for h in range(halves_n) for c in range(cols_n)]
    hid_parts = [[] for _ in range(halves_n)]
    downs = [None] * halves_n
    pending = None
    waiting = []
    sent = None

    def land(made):
        prev_h, cur, got = waiting.pop(0)
        if made is not None:
            got, _ = lax.optimization_barrier((got, made))
        hid_parts[prev_h].append(back_b(cur, got))
        if len(hid_parts[prev_h]) == cols_n:
            downs[prev_h] = finish(hid_parts[prev_h])

    for h, c in plan:
        rows = grouped[h].reshape(n_sec * block_rows, width_local)
        if sent is not None:
            rows, _ = lax.optimization_barrier((rows, sent))
        if h > 0 and c == cols_n - 1 and downs[h - 1] is not None:
            rows, _ = lax.optimization_barrier((rows, downs[h - 1]))
        reduced, made, sent = front(rows, slice(c * cols, (c + 1) * cols))
        if len(waiting) == 1:
            land(made)
        if pending is not None:
            prev_h, prev = pending
            prev, _ = lax.optimization_barrier((prev, made))
            waiting.append((prev_h,) + back_a(prev))
        pending = (h, reduced)
    prev_h, prev = pending
    done_downs = tuple(d for d in downs[:prev_h] if d is not None)
    if done_downs:
        prev, _ = lax.optimization_barrier((prev, done_downs))
    waiting.append((prev_h,) + back_a(prev))
    while waiting:
        land(None)
    pieces = [scatter(down_h) for down_h in downs]
    mixed = jnp.take(jnp.stack(pieces), order, axis=1)
    mixed = mixed.reshape(per_t_seq, batch_count, width_local).astype(jnp.float32)
    own_rows = per_t_seq * batch_count
    erased_own = lax.dynamic_slice_in_dim(erased, ten * own_rows, own_rows, 0)
    erased_own = erased_own.reshape(per_t_seq, batch_count, width_local)
    return (erased_own + mixed).astype(jnp.bfloat16)


def solution(mesh):
    in_specs = (
        P(None, None, "section"),
        P("section"),
        P("section", None),
        P("section", None),
        P("section"),
        P("section", "tensor"),
        P("section", "tensor"),
        P("tensor", "section"),
    )
    out_specs = P("tensor", None, "section")
    return jax.shard_map(body, mesh=mesh, in_specs=in_specs, out_specs=out_specs, check_vma=False)
```

```python
import jax
import jax.numpy as jnp
from jax import lax
from jax.sharding import PartitionSpec as P


_COLS = 2


def _stages(n):
    count = n.bit_length() - 1
    assert 1 << count == n
    return count


def _swap(x, axis, n, bit):
    return lax.ppermute(x, axis, perm=[(a, a ^ (1 << bit)) for a in range(n)])


def _all_sum(x, axis, n):
    for bit in range(_stages(n)):
        x = x + _swap(x, axis, n, bit)
    return x


def _scatter_sum(x, axis, n, bit_order):
    count = _stages(n)
    blocks = x.reshape((2,) * count + x.shape[1:])
    for bit in bit_order:
        pos = count - 1 - bit
        pos = pos - sum(1 for done in bit_order[: bit_order.index(bit)] if count - 1 - done < count - 1 - bit)
        keep = lax.index_in_dim(blocks, 0, pos, keepdims=False)
        send = lax.index_in_dim(blocks, 1, pos, keepdims=False)
        got = _swap(send.astype(jnp.bfloat16), axis, n, bit)
        blocks = keep.astype(jnp.float32) + got.astype(jnp.float32)
        if bit != bit_order[-1]:
            blocks = blocks.astype(jnp.bfloat16)
    return blocks


def _pick_chunks(per_t_seq, batch, n_sec):
    for k in (2, 1):
        if per_t_seq % k == 0 and (per_t_seq // k * batch) % n_sec == 0:
            return k
    raise ValueError("no chunking")


def body(
    stream, concept_mean, erase_basis, erase_lift, norm_gain, gate_weight, up_weight, down_weight
):
    seq_rows, batch_count, width_local = stream.shape
    n_sec = lax.axis_size("section")
    n_ten = lax.axis_size("tensor")
    stages = _stages(n_sec)
    sec = lax.axis_index("section")
    ten = lax.axis_index("tensor")
    width = width_local * n_sec
    hidden_local = gate_weight.shape[1]

    local_rows = stream.reshape(seq_rows * batch_count, width_local)
    partial_basis = jnp.dot(local_rows, erase_basis, preferred_element_type=jnp.float32)
    partial_mean = jnp.dot(concept_mean, erase_basis, preferred_element_type=jnp.float32)
    totals = _all_sum(jnp.concatenate([partial_basis, partial_mean[None, :]], axis=0), "section", n_sec)
    coords = totals[:-1] - totals[-1:]
    lift_float = erase_lift.astype(jnp.float32)
    erased = local_rows.astype(jnp.float32) - jnp.dot(
        coords, lift_float.T, precision=lax.Precision.HIGHEST
    )
    squares = _all_sum(jnp.sum(erased * erased, axis=-1), "section", n_sec)
    inv_rms = lax.rsqrt(squares / width + 1e-05)[:, None]
    normed = (erased * inv_rms * norm_gain[None, :]).astype(jnp.bfloat16)

    per_t_seq = seq_rows // n_ten
    halves_n = _pick_chunks(per_t_seq, batch_count, n_sec)
    span = per_t_seq // halves_n
    part_rows = span * batch_count // n_sec
    order = jnp.bitwise_xor(sec, jnp.arange(n_sec, dtype=sec.dtype))
    ten_order = jnp.bitwise_xor(ten, jnp.arange(n_ten, dtype=ten.dtype))
    grouped = normed.reshape(n_ten, halves_n, n_sec, part_rows, width_local)
    grouped = jnp.take(grouped, order, axis=2, mode="clip")
    grouped = grouped.transpose(1, 2, 0, 3, 4)
    block_rows = n_ten * part_rows
    cols_n = _COLS if hidden_local % (_COLS * 128) == 0 else 1
    cols = hidden_local // cols_n

    def front(rows, cut):
        gate_c = jnp.dot(rows, gate_weight[:, cut], preferred_element_type=jnp.float32)
        up_c = jnp.dot(rows, up_weight[:, cut], preferred_element_type=jnp.float32)
        cur = jnp.concatenate([gate_c.astype(jnp.bfloat16), up_c.astype(jnp.bfloat16)], axis=-1)
        made = cur
        cur = cur.reshape(n_sec, block_rows, 2 * cols)
        first = None
        for bit in range(stages):
            halves = cur.reshape(cur.shape[0] // 2, 2, block_rows, 2 * cols)
            if bit == stages - 1:
                first = halves[:, 1]
            got = _swap(halves[:, 1], "section", n_sec, bit)
            cur = halves[:, 0].astype(jnp.float32) + got.astype(jnp.float32)
            if bit < stages - 1:
                cur = cur.astype(jnp.bfloat16)
        return cur[0], made, first

    def back_a(cur):
        hid = (jax.nn.silu(cur[:, :cols]) * cur[:, cols:]).astype(jnp.bfloat16)
        cur = hid[None]
        return cur, _swap(cur, "section", n_sec, stages - 1)

    def back_b(cur, got):
        cur = jnp.stack([cur, got], axis=1).reshape(2 * cur.shape[0], block_rows, cols)
        for bit in reversed(range(stages - 1)):
            got = _swap(cur, "section", n_sec, bit)
            cur = jnp.stack([cur, got], axis=1).reshape(2 * cur.shape[0], block_rows, cols)
        return cur.reshape(n_sec, n_ten, part_rows, cols)

    def finish(hid_parts):
        hid_all = jnp.take(jnp.concatenate(hid_parts, axis=-1), ten_order, axis=1, mode="clip")
        hid_all = hid_all.transpose(1, 0, 2, 3).reshape(n_ten * n_sec * part_rows, hidden_local)
        half_w = width_local // 2
        outs = []
        for w in range(2):
            acc = jnp.dot(
                hid_all, down_weight[:, w * half_w : (w + 1) * half_w], preferred_element_type=jnp.float32
            )
            outs.append(acc.astype(jnp.bfloat16).reshape(n_ten, n_sec * part_rows, half_w))
        return tuple(outs)

    def scatter(down_h):
        bits = list(range(_stages(n_ten)))
        other = bits[1:2] + bits[:1] + bits[2:]
        piece = jnp.concatenate(
            [
                _scatter_sum(down_h[0], "tensor", n_ten, bits),
                _scatter_sum(down_h[1], "tensor", n_ten, other),
            ],
            axis=-1,
        )
        return piece.reshape(n_sec, part_rows, width_local)

    plan = [(h, c) for h in range(halves_n) for c in range(cols_n)]
    hid_parts = [[] for _ in range(halves_n)]
    downs = [None] * halves_n
    pending = None
    waiting = []
    sent = None

    def land(made):
        prev_h, cur, got = waiting.pop(0)
        if made is not None:
            got, _ = lax.optimization_barrier((got, made))
        hid_parts[prev_h].append(back_b(cur, got))
        if len(hid_parts[prev_h]) == cols_n:
            downs[prev_h] = finish(hid_parts[prev_h])

    for h, c in plan:
        rows = grouped[h].reshape(n_sec * block_rows, width_local)
        if sent is not None:
            rows, _ = lax.optimization_barrier((rows, sent))
        if h > 0 and c == cols_n - 1 and downs[h - 1] is not None:
            rows, _ = lax.optimization_barrier((rows, downs[h - 1]))
        reduced, made, sent = front(rows, slice(c * cols, (c + 1) * cols))
        if len(waiting) == 1:
            land(made)
        if pending is not None:
            prev_h, prev = pending
            prev, _ = lax.optimization_barrier((prev, made))
            waiting.append((prev_h,) + back_a(prev))
        pending = (h, reduced)
    prev_h, prev = pending
    done_downs = tuple(d for d in downs[:prev_h] if d is not None)
    if done_downs:
        prev, _ = lax.optimization_barrier((prev, done_downs))
    waiting.append((prev_h,) + back_a(prev))
    while waiting:
        land(None)
    pieces = [scatter(down_h) for down_h in downs]
    mixed = jnp.take(jnp.stack(pieces), order, axis=1, mode="clip")
    mixed = mixed.reshape(per_t_seq, batch_count, width_local).astype(jnp.float32)
    own_rows = per_t_seq * batch_count
    erased_own = lax.dynamic_slice_in_dim(erased, ten * own_rows, own_rows, 0)
    erased_own = erased_own.reshape(per_t_seq, batch_count, width_local)
    return (erased_own + mixed).astype(jnp.bfloat16)


def solution(mesh):
    in_specs = (
        P(None, None, "section"),
        P("section"),
        P("section", None),
        P("section", None),
        P("section"),
        P("section", "tensor"),
        P("section", "tensor"),
        P("tensor", "section"),
    )
    out_specs = P("tensor", None, "section")
    return jax.shard_map(body, mesh=mesh, in_specs=in_specs, out_specs=out_specs, check_vma=False)
```

```python
import jax
import jax.numpy as jnp
from jax import lax
from jax.sharding import PartitionSpec as P


_COLS = 2


def _stages(n):
    count = n.bit_length() - 1
    assert 1 << count == n
    return count


def _swap(x, axis, n, bit):
    return lax.ppermute(x, axis, perm=[(a, a ^ (1 << bit)) for a in range(n)])


def _all_sum(x, axis, n):
    for bit in range(_stages(n)):
        x = x + _swap(x, axis, n, bit)
    return x


def _scatter_sum(x, axis, n, bit_order):
    count = _stages(n)
    blocks = x.reshape((2,) * count + x.shape[1:])
    for bit in bit_order:
        pos = count - 1 - bit
        pos = pos - sum(1 for done in bit_order[: bit_order.index(bit)] if count - 1 - done < count - 1 - bit)
        keep = lax.index_in_dim(blocks, 0, pos, keepdims=False)
        send = lax.index_in_dim(blocks, 1, pos, keepdims=False)
        got = _swap(send.astype(jnp.bfloat16), axis, n, bit)
        blocks = keep.astype(jnp.float32) + got.astype(jnp.float32)
        if bit != bit_order[-1]:
            blocks = blocks.astype(jnp.bfloat16)
    return blocks


def _pick_chunks(per_t_seq, batch, n_sec):
    for k in (2, 1):
        if per_t_seq % k == 0 and (per_t_seq // k * batch) % n_sec == 0:
            return k
    raise ValueError("no chunking")


def body(
    stream, concept_mean, erase_basis, erase_lift, norm_gain, gate_weight, up_weight, down_weight
):
    seq_rows, batch_count, width_local = stream.shape
    n_sec = lax.axis_size("section")
    n_ten = lax.axis_size("tensor")
    stages = _stages(n_sec)
    sec = lax.axis_index("section")
    ten = lax.axis_index("tensor")
    width = width_local * n_sec
    hidden_local = gate_weight.shape[1]

    per_t_seq = seq_rows // n_ten
    halves_n = _pick_chunks(per_t_seq, batch_count, n_sec)
    span = per_t_seq // halves_n
    part_rows = span * batch_count // n_sec
    order = jnp.bitwise_xor(sec, jnp.arange(n_sec, dtype=sec.dtype))
    ten_order = jnp.bitwise_xor(ten, jnp.arange(n_ten, dtype=ten.dtype))
    block_rows = n_ten * part_rows
    cols_n = _COLS if hidden_local % (_COLS * 128) == 0 else 1
    cols = hidden_local // cols_n

    split_rows = stream.reshape(n_ten, halves_n, span * batch_count, width_local)
    partial_mean = jnp.dot(concept_mean, erase_basis, preferred_element_type=jnp.float32)
    lift_float = erase_lift.astype(jnp.float32)
    grouped = []
    erased_own = []
    mean_total = None
    for h in range(halves_n):
        rows_h = split_rows[:, h].reshape(n_ten * span * batch_count, width_local)
        partial_basis = jnp.dot(rows_h, erase_basis, preferred_element_type=jnp.float32)
        if mean_total is None:
            totals = _all_sum(
                jnp.concatenate([partial_basis, partial_mean[None, :]], axis=0), "section", n_sec
            )
            mean_total = totals[-1:]
            totals = totals[:-1]
        else:
            totals = _all_sum(partial_basis, "section", n_sec)
        coords = totals - mean_total
        erased = rows_h.astype(jnp.float32) - jnp.dot(
            coords, lift_float.T, precision=lax.Precision.HIGHEST
        )
        squares = _all_sum(jnp.sum(erased * erased, axis=-1), "section", n_sec)
        inv_rms = lax.rsqrt(squares / width + 1e-05)[:, None]
        normed = (erased * inv_rms * norm_gain[None, :]).astype(jnp.bfloat16)
        normed = jnp.take(normed.reshape(n_ten, n_sec, part_rows, width_local), order, axis=1)
        grouped.append(normed.transpose(1, 0, 2, 3))
        erased_own.append(
            lax.dynamic_index_in_dim(
                erased.reshape(n_ten, span * batch_count, width_local), ten, 0, keepdims=False
            )
        )

    def front(rows, cut):
        gate_c = jnp.dot(rows, gate_weight[:, cut], preferred_element_type=jnp.float32)
        up_c = jnp.dot(rows, up_weight[:, cut], preferred_element_type=jnp.float32)
        cur = jnp.concatenate([gate_c.astype(jnp.bfloat16), up_c.astype(jnp.bfloat16)], axis=-1)
        made = cur
        cur = cur.reshape(n_sec, block_rows, 2 * cols)
        first = None
        for bit in range(stages):
            halves = cur.reshape(cur.shape[0] // 2, 2, block_rows, 2 * cols)
            if bit == stages - 1:
                first = halves[:, 1]
            got = _swap(halves[:, 1], "section", n_sec, bit)
            cur = halves[:, 0].astype(jnp.float32) + got.astype(jnp.float32)
            if bit < stages - 1:
                cur = cur.astype(jnp.bfloat16)
        return cur[0], made, first

    def back_a(cur):
        hid = (jax.nn.silu(cur[:, :cols]) * cur[:, cols:]).astype(jnp.bfloat16)
        cur = hid[None]
        return cur, _swap(cur, "section", n_sec, stages - 1)

    def back_b(cur, got):
        cur = jnp.stack([cur, got], axis=1).reshape(2 * cur.shape[0], block_rows, cols)
        for bit in reversed(range(stages - 1)):
            got = _swap(cur, "section", n_sec, bit)
            cur = jnp.stack([cur, got], axis=1).reshape(2 * cur.shape[0], block_rows, cols)
        return cur.reshape(n_sec, n_ten, part_rows, cols)

    def finish(hid_parts):
        hid_all = jnp.take(jnp.concatenate(hid_parts, axis=-1), ten_order, axis=1)
        hid_all = hid_all.transpose(1, 0, 2, 3).reshape(n_ten * n_sec * part_rows, hidden_local)
        acc = jnp.dot(hid_all, down_weight, preferred_element_type=jnp.float32)
        return acc.astype(jnp.bfloat16).reshape(n_ten, n_sec * part_rows, width_local)

    def scatter(down_h):
        bits = list(range(_stages(n_ten)))
        other = bits[1:2] + bits[:1] + bits[2:]
        half_w = width_local // 2
        piece = jnp.concatenate(
            [
                _scatter_sum(down_h[..., :half_w], "tensor", n_ten, bits),
                _scatter_sum(down_h[..., half_w:], "tensor", n_ten, other),
            ],
            axis=-1,
        )
        return piece.reshape(n_sec, part_rows, width_local)

    plan = [(h, c) for h in range(halves_n) for c in range(cols_n)]
    hid_parts = [[] for _ in range(halves_n)]
    downs = [None] * halves_n
    pending = None
    waiting = []
    sent = None

    def land(made):
        prev_h, cur, got = waiting.pop(0)
        if made is not None:
            got, _ = lax.optimization_barrier((got, made))
        hid_parts[prev_h].append(back_b(cur, got))
        if len(hid_parts[prev_h]) == cols_n:
            downs[prev_h] = finish(hid_parts[prev_h])

    for h, c in plan:
        rows = grouped[h].reshape(n_sec * block_rows, width_local)
        if sent is not None:
            rows, _ = lax.optimization_barrier((rows, sent))
        if h > 0 and c == cols_n - 1 and downs[h - 1] is not None:
            rows, _ = lax.optimization_barrier((rows, downs[h - 1]))
        reduced, made, sent = front(rows, slice(c * cols, (c + 1) * cols))
        if len(waiting) == 1:
            land(made)
        if pending is not None:
            prev_h, prev = pending
            prev, _ = lax.optimization_barrier((prev, made))
            waiting.append((prev_h,) + back_a(prev))
        pending = (h, reduced)
    prev_h, prev = pending
    done_downs = tuple(d for d in downs[:prev_h] if d is not None)
    if done_downs:
        prev, _ = lax.optimization_barrier((prev, done_downs))
    waiting.append((prev_h,) + back_a(prev))
    while waiting:
        land(None)
    pieces = [scatter(down_h) for down_h in downs]
    mixed = jnp.take(jnp.stack(pieces), order, axis=1)
    mixed = mixed.reshape(per_t_seq, batch_count, width_local).astype(jnp.float32)
    own = jnp.stack(erased_own).reshape(per_t_seq, batch_count, width_local)
    return (own + mixed).astype(jnp.bfloat16)


def solution(mesh):
    in_specs = (
        P(None, None, "section"),
        P("section"),
        P("section", None),
        P("section", None),
        P("section"),
        P("section", "tensor"),
        P("section", "tensor"),
        P("tensor", "section"),
    )
    out_specs = P("tensor", None, "section")
    return jax.shard_map(body, mesh=mesh, in_specs=in_specs, out_specs=out_specs, check_vma=False)
```

```python
import jax
import jax.numpy as jnp
from jax import lax
from jax.sharding import PartitionSpec as P


_COLS = 2


def _stages(n):
    count = n.bit_length() - 1
    assert 1 << count == n
    return count


def _swap(x, axis, n, bit):
    return lax.ppermute(x, axis, perm=[(a, a ^ (1 << bit)) for a in range(n)])


def _all_sum(x, axis, n):
    for bit in range(_stages(n)):
        x = x + _swap(x, axis, n, bit)
    return x


def _scatter_sum(x, axis, n, bit_order):
    count = _stages(n)
    blocks = x.reshape((2,) * count + x.shape[1:])
    for bit in bit_order:
        pos = count - 1 - bit
        pos = pos - sum(1 for done in bit_order[: bit_order.index(bit)] if count - 1 - done < count - 1 - bit)
        keep = lax.index_in_dim(blocks, 0, pos, keepdims=False)
        send = lax.index_in_dim(blocks, 1, pos, keepdims=False)
        got = _swap(send.astype(jnp.bfloat16), axis, n, bit)
        blocks = keep.astype(jnp.float32) + got.astype(jnp.float32)
        if bit != bit_order[-1]:
            blocks = blocks.astype(jnp.bfloat16)
    return blocks


def _pick_chunks(per_t_seq, batch, n_sec):
    for k in (2, 1):
        if per_t_seq % k == 0 and (per_t_seq // k * batch) % n_sec == 0:
            return k
    raise ValueError("no chunking")


def body(
    stream, concept_mean, erase_basis, erase_lift, norm_gain, gate_weight, up_weight, down_weight
):
    seq_rows, batch_count, width_local = stream.shape
    n_sec = lax.axis_size("section")
    n_ten = lax.axis_size("tensor")
    stages = _stages(n_sec)
    sec = lax.axis_index("section")
    ten = lax.axis_index("tensor")
    width = width_local * n_sec
    hidden_local = gate_weight.shape[1]

    per_t_seq = seq_rows // n_ten
    halves_n = _pick_chunks(per_t_seq, batch_count, n_sec)
    span = per_t_seq // halves_n
    part_rows = span * batch_count // n_sec
    order = jnp.bitwise_xor(sec, jnp.arange(n_sec, dtype=sec.dtype))
    ten_order = jnp.bitwise_xor(ten, jnp.arange(n_ten, dtype=ten.dtype))
    block_rows = n_ten * part_rows
    cols_n = _COLS if hidden_local % (_COLS * 128) == 0 else 1
    cols = hidden_local // cols_n

    split_rows = stream.reshape(n_ten, halves_n, span * batch_count, width_local)
    partial_mean = jnp.dot(concept_mean, erase_basis, preferred_element_type=jnp.float32)
    lift_float = erase_lift.astype(jnp.float32)
    grouped = [None] * halves_n
    erased_own = [None] * halves_n
    mean_total = []

    def prelude(h, tie):
        rows_h = split_rows[:, h].reshape(n_ten * span * batch_count, width_local)
        if tie is not None:
            rows_h, _ = lax.optimization_barrier((rows_h, tie))
        partial_basis = jnp.dot(rows_h, erase_basis, preferred_element_type=jnp.float32)
        if not mean_total:
            totals = _all_sum(
                jnp.concatenate([partial_basis, partial_mean[None, :]], axis=0), "section", n_sec
            )
            mean_total.append(totals[-1:])
            totals = totals[:-1]
        else:
            totals = _all_sum(partial_basis, "section", n_sec)
        coords = totals - mean_total[0]
        erased = rows_h.astype(jnp.float32) - jnp.dot(
            coords, lift_float.T, precision=lax.Precision.HIGHEST
        )
        squares = _all_sum(jnp.sum(erased * erased, axis=-1), "section", n_sec)
        inv_rms = lax.rsqrt(squares / width + 1e-05)[:, None]
        normed = (erased * inv_rms * norm_gain[None, :]).astype(jnp.bfloat16)
        normed = jnp.take(normed.reshape(n_ten, n_sec, part_rows, width_local), order, axis=1)
        grouped[h] = normed.transpose(1, 0, 2, 3)
        erased_own[h] = lax.dynamic_index_in_dim(
            erased.reshape(n_ten, span * batch_count, width_local), ten, 0, keepdims=False
        )

    def front(rows, cut):
        gate_c = jnp.dot(rows, gate_weight[:, cut], preferred_element_type=jnp.float32)
        up_c = jnp.dot(rows, up_weight[:, cut], preferred_element_type=jnp.float32)
        cur = jnp.concatenate([gate_c.astype(jnp.bfloat16), up_c.astype(jnp.bfloat16)], axis=-1)
        made = cur
        cur = cur.reshape(n_sec, block_rows, 2 * cols)
        first = None
        for bit in range(stages):
            halves = cur.reshape(cur.shape[0] // 2, 2, block_rows, 2 * cols)
            if bit == stages - 1:
                first = halves[:, 1]
            got = _swap(halves[:, 1], "section", n_sec, bit)
            cur = halves[:, 0].astype(jnp.float32) + got.astype(jnp.float32)
            if bit < stages - 1:
                cur = cur.astype(jnp.bfloat16)
        return cur[0], made, first

    def back_a(cur):
        hid = (jax.nn.silu(cur[:, :cols]) * cur[:, cols:]).astype(jnp.bfloat16)
        cur = hid[None]
        return cur, _swap(cur, "section", n_sec, stages - 1)

    def back_b(cur, got):
        cur = jnp.stack([cur, got], axis=1).reshape(2 * cur.shape[0], block_rows, cols)
        for bit in reversed(range(stages - 1)):
            got = _swap(cur, "section", n_sec, bit)
            cur = jnp.stack([cur, got], axis=1).reshape(2 * cur.shape[0], block_rows, cols)
        return cur.reshape(n_sec, n_ten, part_rows, cols)

    def finish(hid_parts):
        hid_all = jnp.take(jnp.concatenate(hid_parts, axis=-1), ten_order, axis=1)
        hid_all = hid_all.transpose(1, 0, 2, 3).reshape(n_ten * n_sec * part_rows, hidden_local)
        acc = jnp.dot(hid_all, down_weight, preferred_element_type=jnp.float32)
        return acc.astype(jnp.bfloat16).reshape(n_ten, n_sec * part_rows, width_local)

    def scatter(down_h):
        bits = list(range(_stages(n_ten)))
        other = bits[1:2] + bits[:1] + bits[2:]
        half_w = width_local // 2
        piece = jnp.concatenate(
            [
                _scatter_sum(down_h[..., :half_w], "tensor", n_ten, bits),
                _scatter_sum(down_h[..., half_w:], "tensor", n_ten, other),
            ],
            axis=-1,
        )
        return piece.reshape(n_sec, part_rows, width_local)

    plan = [(h, c) for h in range(halves_n) for c in range(cols_n)]
    hid_parts = [[] for _ in range(halves_n)]
    downs = [None] * halves_n
    pending = None
    waiting = []
    sent = None

    def land(made):
        prev_h, cur, got = waiting.pop(0)
        if made is not None:
            got, _ = lax.optimization_barrier((got, made))
        hid_parts[prev_h].append(back_b(cur, got))
        if len(hid_parts[prev_h]) == cols_n:
            downs[prev_h] = finish(hid_parts[prev_h])

    made = None
    for h, c in plan:
        if grouped[h] is None:
            prelude(h, made)
        rows = grouped[h].reshape(n_sec * block_rows, width_local)
        if sent is not None:
            rows, _ = lax.optimization_barrier((rows, sent))
        if h > 0 and c == cols_n - 1 and downs[h - 1] is not None:
            rows, _ = lax.optimization_barrier((rows, downs[h - 1]))
        reduced, made, sent = front(rows, slice(c * cols, (c + 1) * cols))
        if len(waiting) == 1:
            land(made)
        if pending is not None:
            prev_h, prev = pending
            prev, _ = lax.optimization_barrier((prev, made))
            waiting.append((prev_h,) + back_a(prev))
        pending = (h, reduced)
    prev_h, prev = pending
    done_downs = tuple(d for d in downs[:prev_h] if d is not None)
    if done_downs:
        prev, _ = lax.optimization_barrier((prev, done_downs))
    waiting.append((prev_h,) + back_a(prev))
    while waiting:
        land(None)
    pieces = [scatter(down_h) for down_h in downs]
    mixed = jnp.take(jnp.stack(pieces), order, axis=1)
    mixed = mixed.reshape(per_t_seq, batch_count, width_local).astype(jnp.float32)
    own = jnp.stack(erased_own).reshape(per_t_seq, batch_count, width_local)
    return (own + mixed).astype(jnp.bfloat16)


def solution(mesh):
    in_specs = (
        P(None, None, "section"),
        P("section"),
        P("section", None),
        P("section", None),
        P("section"),
        P("section", "tensor"),
        P("section", "tensor"),
        P("tensor", "section"),
    )
    out_specs = P("tensor", None, "section")
    return jax.shard_map(body, mesh=mesh, in_specs=in_specs, out_specs=out_specs, check_vma=False)
```

```python
import jax
import jax.numpy as jnp
from jax import lax
from jax.sharding import PartitionSpec as P


_COLS = 2


def _stages(n):
    count = n.bit_length() - 1
    assert 1 << count == n
    return count


def _swap(x, axis, n, bit):
    return lax.ppermute(x, axis, perm=[(a, a ^ (1 << bit)) for a in range(n)])


def _all_sum(x, axis, n):
    for bit in range(_stages(n)):
        x = x + _swap(x, axis, n, bit)
    return x


def _scatter_sum(x, axis, n, bit_order):
    count = _stages(n)
    blocks = x.reshape((2,) * count + x.shape[1:])
    for bit in bit_order:
        pos = count - 1 - bit
        pos = pos - sum(1 for done in bit_order[: bit_order.index(bit)] if count - 1 - done < count - 1 - bit)
        keep = lax.index_in_dim(blocks, 0, pos, keepdims=False)
        send = lax.index_in_dim(blocks, 1, pos, keepdims=False)
        got = _swap(send.astype(jnp.bfloat16), axis, n, bit)
        blocks = keep.astype(jnp.float32) + got.astype(jnp.float32)
        if bit != bit_order[-1]:
            blocks = blocks.astype(jnp.bfloat16)
    return blocks


def _pick_spans(per_t_seq, batch, n_sec):
    first = per_t_seq * 5 // 8
    if first % n_sec == 0 and (per_t_seq - first) % n_sec == 0 and first * batch % n_sec == 0:
        return [first, per_t_seq - first]
    count = _pick_chunks(per_t_seq, batch, n_sec)
    return [per_t_seq // count] * count


def _pick_chunks(per_t_seq, batch, n_sec):
    for k in (2, 1):
        if per_t_seq % k == 0 and (per_t_seq // k * batch) % n_sec == 0:
            return k
    raise ValueError("no chunking")


def body(
    stream, concept_mean, erase_basis, erase_lift, norm_gain, gate_weight, up_weight, down_weight
):
    seq_rows, batch_count, width_local = stream.shape
    n_sec = lax.axis_size("section")
    n_ten = lax.axis_size("tensor")
    stages = _stages(n_sec)
    sec = lax.axis_index("section")
    ten = lax.axis_index("tensor")
    width = width_local * n_sec
    hidden_local = gate_weight.shape[1]

    local_rows = stream.reshape(seq_rows * batch_count, width_local)
    partial_basis = jnp.dot(local_rows, erase_basis, preferred_element_type=jnp.float32)
    partial_mean = jnp.dot(concept_mean, erase_basis, preferred_element_type=jnp.float32)
    totals = _all_sum(jnp.concatenate([partial_basis, partial_mean[None, :]], axis=0), "section", n_sec)
    coords = totals[:-1] - totals[-1:]
    lift_float = erase_lift.astype(jnp.float32)
    erased = local_rows.astype(jnp.float32) - jnp.dot(
        coords, lift_float.T, precision=lax.Precision.HIGHEST
    )
    squares = _all_sum(jnp.sum(erased * erased, axis=-1), "section", n_sec)
    inv_rms = lax.rsqrt(squares / width + 1e-05)[:, None]
    normed = (erased * inv_rms * norm_gain[None, :]).astype(jnp.bfloat16)

    per_t_seq = seq_rows // n_ten
    spans = _pick_spans(per_t_seq, batch_count, n_sec)
    halves_n = len(spans)
    order = jnp.bitwise_xor(sec, jnp.arange(n_sec, dtype=sec.dtype))
    ten_order = jnp.bitwise_xor(ten, jnp.arange(n_ten, dtype=ten.dtype))
    by_ten = normed.reshape(n_ten, per_t_seq * batch_count, width_local)
    grouped = []
    parts = []
    offset = 0
    for span in spans:
        part_rows = span * batch_count // n_sec
        piece = by_ten[:, offset : offset + span * batch_count]
        offset += span * batch_count
        piece = jnp.take(piece.reshape(n_ten, n_sec, part_rows, width_local), order, axis=1)
        grouped.append(piece.transpose(1, 0, 2, 3))
        parts.append(part_rows)
    cols_n = _COLS if hidden_local % (_COLS * 128) == 0 else 1
    cols = hidden_local // cols_n

    def front(rows, cut, part_rows):
        block_rows = n_ten * part_rows
        gate_c = jnp.dot(rows, gate_weight[:, cut], preferred_element_type=jnp.float32)
        up_c = jnp.dot(rows, up_weight[:, cut], preferred_element_type=jnp.float32)
        cur = jnp.concatenate([gate_c.astype(jnp.bfloat16), up_c.astype(jnp.bfloat16)], axis=-1)
        made = cur
        cur = cur.reshape(n_sec, block_rows, 2 * cols)
        first = None
        for bit in range(stages):
            halves = cur.reshape(cur.shape[0] // 2, 2, block_rows, 2 * cols)
            if bit == stages - 1:
                first = halves[:, 1]
            got = _swap(halves[:, 1], "section", n_sec, bit)
            cur = halves[:, 0].astype(jnp.float32) + got.astype(jnp.float32)
            if bit < stages - 1:
                cur = cur.astype(jnp.bfloat16)
        return cur[0], made, first

    def back_a(cur):
        hid = (jax.nn.silu(cur[:, :cols]) * cur[:, cols:]).astype(jnp.bfloat16)
        cur = hid[None]
        return cur, _swap(cur, "section", n_sec, stages - 1)

    def back_b(cur, got):
        cur = jnp.stack([cur, got], axis=1).reshape(2 * cur.shape[0], cur.shape[1], cols)
        for bit in reversed(range(stages - 1)):
            got = _swap(cur, "section", n_sec, bit)
            cur = jnp.stack([cur, got], axis=1).reshape(2 * cur.shape[0], cur.shape[1], cols)
        return cur.reshape(n_sec, n_ten, -1, cols)

    def finish(hid_parts):
        hid_all = jnp.take(jnp.concatenate(hid_parts, axis=-1), ten_order, axis=1)
        hid_all = hid_all.transpose(1, 0, 2, 3).reshape(-1, hidden_local)
        acc = jnp.dot(hid_all, down_weight, preferred_element_type=jnp.float32)
        return acc.astype(jnp.bfloat16).reshape(n_ten, -1, width_local)

    def scatter(down_h):
        bits = list(range(_stages(n_ten)))
        other = bits[1:2] + bits[:1] + bits[2:]
        half_w = width_local // 2
        piece = jnp.concatenate(
            [
                _scatter_sum(down_h[..., :half_w], "tensor", n_ten, bits),
                _scatter_sum(down_h[..., half_w:], "tensor", n_ten, other),
            ],
            axis=-1,
        )
        return piece.reshape(n_sec, -1, width_local)

    plan = [(h, c) for h in range(halves_n) for c in range(cols_n)]
    hid_parts = [[] for _ in range(halves_n)]
    downs = [None] * halves_n
    pending = None
    waiting = []
    sent = None

    def land(made):
        prev_h, cur, got = waiting.pop(0)
        if made is not None:
            got, _ = lax.optimization_barrier((got, made))
        hid_parts[prev_h].append(back_b(cur, got))
        if len(hid_parts[prev_h]) == cols_n:
            downs[prev_h] = finish(hid_parts[prev_h])

    for h, c in plan:
        rows = grouped[h].reshape(-1, width_local)
        if sent is not None:
            rows, _ = lax.optimization_barrier((rows, sent))
        if h > 0 and c == cols_n - 1 and downs[h - 1] is not None:
            rows, _ = lax.optimization_barrier((rows, downs[h - 1]))
        reduced, made, sent = front(rows, slice(c * cols, (c + 1) * cols), parts[h])
        if len(waiting) == 1:
            land(made)
        if pending is not None:
            prev_h, prev = pending
            prev, _ = lax.optimization_barrier((prev, made))
            waiting.append((prev_h,) + back_a(prev))
        pending = (h, reduced)
    prev_h, prev = pending
    done_downs = tuple(d for d in downs[:prev_h] if d is not None)
    if done_downs:
        prev, _ = lax.optimization_barrier((prev, done_downs))
    waiting.append((prev_h,) + back_a(prev))
    while waiting:
        land(None)
    pieces = [scatter(down_h) for down_h in downs]
    mixed = jnp.concatenate(
        [
            jnp.take(piece, order, axis=0).reshape(span, batch_count, width_local)
            for piece, span in zip(pieces, spans)
        ],
        axis=0,
    ).astype(jnp.float32)
    own_rows = per_t_seq * batch_count
    erased_own = lax.dynamic_slice_in_dim(erased, ten * own_rows, own_rows, 0)
    erased_own = erased_own.reshape(per_t_seq, batch_count, width_local)
    return (erased_own + mixed).astype(jnp.bfloat16)


def solution(mesh):
    in_specs = (
        P(None, None, "section"),
        P("section"),
        P("section", None),
        P("section", None),
        P("section"),
        P("section", "tensor"),
        P("section", "tensor"),
        P("tensor", "section"),
    )
    out_specs = P("tensor", None, "section")
    return jax.shard_map(body, mesh=mesh, in_specs=in_specs, out_specs=out_specs, check_vma=False)
```

```python
import jax
import jax.numpy as jnp
from jax import lax
from jax.sharding import PartitionSpec as P


_COLS = 2


def _stages(n):
    count = n.bit_length() - 1
    assert 1 << count == n
    return count


def _swap(x, axis, n, bit):
    return lax.ppermute(x, axis, perm=[(a, a ^ (1 << bit)) for a in range(n)])


def _all_sum(x, axis, n):
    for bit in range(_stages(n)):
        x = x + _swap(x, axis, n, bit)
    return x


def _scatter_sum(x, axis, n, bit_order, me):
    count = _stages(n)
    blocks = x.reshape(x.shape[:1] + (2,) * count + x.shape[2:])
    for bit in bit_order:
        pos = 1 + count - 1 - bit
        pos = pos - sum(1 for done in bit_order[: bit_order.index(bit)] if done > bit)
        mine = (me >> bit) & 1
        keep = lax.dynamic_index_in_dim(blocks, mine, pos, keepdims=False)
        send = lax.dynamic_index_in_dim(blocks, 1 - mine, pos, keepdims=False)
        got = _swap(send.astype(jnp.bfloat16), axis, n, bit)
        blocks = keep.astype(jnp.float32) + got.astype(jnp.float32)
        if bit != bit_order[-1]:
            blocks = blocks.astype(jnp.bfloat16)
    return blocks


def _pick_chunks(per_t_seq, batch, n_sec):
    for k in (2, 1):
        if per_t_seq % k == 0 and (per_t_seq // k * batch) % n_sec == 0:
            return k
    raise ValueError("no chunking")


def body(
    stream, concept_mean, erase_basis, erase_lift, norm_gain, gate_weight, up_weight, down_weight
):
    seq_rows, batch_count, width_local = stream.shape
    n_sec = lax.axis_size("section")
    n_ten = lax.axis_size("tensor")
    stages = _stages(n_sec)
    sec = lax.axis_index("section")
    ten = lax.axis_index("tensor")
    width = width_local * n_sec
    hidden_local = gate_weight.shape[1]

    local_rows = stream.reshape(seq_rows * batch_count, width_local)
    partial_basis = jnp.dot(local_rows, erase_basis, preferred_element_type=jnp.float32)
    partial_mean = jnp.dot(concept_mean, erase_basis, preferred_element_type=jnp.float32)
    totals = _all_sum(jnp.concatenate([partial_basis, partial_mean[None, :]], axis=0), "section", n_sec)
    coords = totals[:-1] - totals[-1:]
    lift_float = erase_lift.astype(jnp.float32)
    erased = local_rows.astype(jnp.float32) - jnp.dot(
        coords, lift_float.T, precision=lax.Precision.HIGHEST
    )
    squares = _all_sum(jnp.sum(erased * erased, axis=-1), "section", n_sec)
    inv_rms = lax.rsqrt(squares / width + 1e-05)[:, None]
    normed = (erased * inv_rms * norm_gain[None, :]).astype(jnp.bfloat16)

    per_t_seq = seq_rows // n_ten
    halves_n = _pick_chunks(per_t_seq, batch_count, n_sec)
    span = per_t_seq // halves_n
    part_rows = span * batch_count // n_sec
    order = jnp.bitwise_xor(sec, jnp.arange(n_sec, dtype=sec.dtype))
    grouped = normed.reshape(n_ten, halves_n, n_sec, part_rows, width_local)
    grouped = jnp.take(grouped, order, axis=2)
    grouped = grouped.transpose(1, 2, 0, 3, 4)
    block_rows = n_ten * part_rows
    cols_n = _COLS if hidden_local % (_COLS * 128) == 0 else 1
    cols = hidden_local // cols_n

    def front(rows, cut):
        gate_c = jnp.dot(rows, gate_weight[:, cut], preferred_element_type=jnp.float32)
        up_c = jnp.dot(rows, up_weight[:, cut], preferred_element_type=jnp.float32)
        cur = jnp.concatenate([gate_c.astype(jnp.bfloat16), up_c.astype(jnp.bfloat16)], axis=-1)
        made = cur
        cur = cur.reshape(n_sec, block_rows, 2 * cols)
        first = None
        for bit in range(stages):
            halves = cur.reshape(cur.shape[0] // 2, 2, block_rows, 2 * cols)
            if bit == stages - 1:
                first = halves[:, 1]
            got = _swap(halves[:, 1], "section", n_sec, bit)
            cur = halves[:, 0].astype(jnp.float32) + got.astype(jnp.float32)
            if bit < stages - 1:
                cur = cur.astype(jnp.bfloat16)
        return cur[0], made, first

    def back_a(cur):
        hid = (jax.nn.silu(cur[:, :cols]) * cur[:, cols:]).astype(jnp.bfloat16)
        cur = hid[None]
        return cur, _swap(cur, "section", n_sec, stages - 1)

    def back_b(cur, got):
        cur = jnp.stack([cur, got], axis=1).reshape(2 * cur.shape[0], block_rows, cols)
        for bit in reversed(range(stages - 1)):
            got = _swap(cur, "section", n_sec, bit)
            cur = jnp.stack([cur, got], axis=1).reshape(2 * cur.shape[0], block_rows, cols)
        return cur.reshape(n_sec, n_ten, part_rows, cols)

    def finish(hid_parts):
        hid_all = jnp.concatenate(hid_parts, axis=-1).reshape(-1, hidden_local)
        acc = jnp.dot(hid_all, down_weight, preferred_element_type=jnp.float32)
        return acc.astype(jnp.bfloat16).reshape(n_sec, n_ten, part_rows, width_local)

    def scatter(down_h):
        bits = list(range(_stages(n_ten)))
        other = bits[1:2] + bits[:1] + bits[2:]
        half_w = width_local // 2
        piece = jnp.concatenate(
            [
                _scatter_sum(down_h[..., :half_w], "tensor", n_ten, bits, ten),
                _scatter_sum(down_h[..., half_w:], "tensor", n_ten, other, ten),
            ],
            axis=-1,
        )
        return piece.reshape(n_sec, part_rows, width_local)

    plan = [(h, c) for h in range(halves_n) for c in range(cols_n)]
    hid_parts = [[] for _ in range(halves_n)]
    downs = [None] * halves_n
    pending = None
    waiting = []
    sent = None

    def land(made):
        prev_h, cur, got = waiting.pop(0)
        if made is not None:
            got, _ = lax.optimization_barrier((got, made))
        hid_parts[prev_h].append(back_b(cur, got))
        if len(hid_parts[prev_h]) == cols_n:
            downs[prev_h] = finish(hid_parts[prev_h])

    for h, c in plan:
        rows = grouped[h].reshape(n_sec * block_rows, width_local)
        if sent is not None:
            rows, _ = lax.optimization_barrier((rows, sent))
        if h > 0 and c == cols_n - 1 and downs[h - 1] is not None:
            rows, _ = lax.optimization_barrier((rows, downs[h - 1]))
        reduced, made, sent = front(rows, slice(c * cols, (c + 1) * cols))
        if len(waiting) == 1:
            land(made)
        if pending is not None:
            prev_h, prev = pending
            prev, _ = lax.optimization_barrier((prev, made))
            waiting.append((prev_h,) + back_a(prev))
        pending = (h, reduced)
    prev_h, prev = pending
    done_downs = tuple(d for d in downs[:prev_h] if d is not None)
    if done_downs:
        prev, _ = lax.optimization_barrier((prev, done_downs))
    waiting.append((prev_h,) + back_a(prev))
    while waiting:
        land(None)
    pieces = [scatter(down_h) for down_h in downs]
    mixed = jnp.take(jnp.stack(pieces), order, axis=1)
    mixed = mixed.reshape(per_t_seq, batch_count, width_local).astype(jnp.float32)
    own_rows = per_t_seq * batch_count
    erased_own = lax.dynamic_slice_in_dim(erased, ten * own_rows, own_rows, 0)
    erased_own = erased_own.reshape(per_t_seq, batch_count, width_local)
    return (erased_own + mixed).astype(jnp.bfloat16)


def solution(mesh):
    in_specs = (
        P(None, None, "section"),
        P("section"),
        P("section", None),
        P("section", None),
        P("section"),
        P("section", "tensor"),
        P("section", "tensor"),
        P("tensor", "section"),
    )
    out_specs = P("tensor", None, "section")
    return jax.shard_map(body, mesh=mesh, in_specs=in_specs, out_specs=out_specs, check_vma=False)
```

```python
import jax
import jax.numpy as jnp
from jax import lax
from jax.sharding import PartitionSpec as P


_COLS = 2


def _stages(n):
    count = n.bit_length() - 1
    assert 1 << count == n
    return count


def _swap(x, axis, n, bit):
    return lax.ppermute(x, axis, perm=[(a, a ^ (1 << bit)) for a in range(n)])


def _all_sum(x, axis, n):
    for bit in range(_stages(n)):
        x = x + _swap(x, axis, n, bit)
    return x


def _scatter_sum(x, axis, n, bit_order, me):
    count = _stages(n)
    blocks = x.reshape(x.shape[:1] + (2,) * count + x.shape[2:])
    for bit in bit_order:
        pos = 1 + count - 1 - bit
        pos = pos - sum(1 for done in bit_order[: bit_order.index(bit)] if done > bit)
        mine = (me >> bit) & 1
        keep = lax.dynamic_index_in_dim(blocks, mine, pos, keepdims=False)
        send = lax.dynamic_index_in_dim(blocks, 1 - mine, pos, keepdims=False)
        got = _swap(send.astype(jnp.bfloat16), axis, n, bit)
        blocks = keep.astype(jnp.float32) + got.astype(jnp.float32)
        if bit != bit_order[-1]:
            blocks = blocks.astype(jnp.bfloat16)
    return blocks


def _pick_chunks(per_t_seq, batch, n_sec):
    for k in (2, 1):
        if per_t_seq % k == 0 and (per_t_seq // k * batch) % n_sec == 0:
            return k
    raise ValueError("no chunking")


def body(
    stream, concept_mean, erase_basis, erase_lift, norm_gain, gate_weight, up_weight, down_weight
):
    seq_rows, batch_count, width_local = stream.shape
    n_sec = lax.axis_size("section")
    n_ten = lax.axis_size("tensor")
    stages = _stages(n_sec)
    sec = lax.axis_index("section")
    ten = lax.axis_index("tensor")
    width = width_local * n_sec
    hidden_local = gate_weight.shape[1]

    local_rows = stream.reshape(seq_rows * batch_count, width_local)
    partial_basis = jnp.dot(local_rows, erase_basis, preferred_element_type=jnp.float32)
    partial_mean = jnp.dot(concept_mean, erase_basis, preferred_element_type=jnp.float32)
    totals = _all_sum(jnp.concatenate([partial_basis, partial_mean[None, :]], axis=0), "section", n_sec)
    coords = totals[:-1] - totals[-1:]
    lift_float = erase_lift.astype(jnp.float32)
    erased = local_rows.astype(jnp.float32) - jnp.dot(
        coords, lift_float.T, precision=lax.Precision.HIGHEST
    )
    squares = _all_sum(jnp.sum(erased * erased, axis=-1), "section", n_sec)
    inv_rms = lax.rsqrt(squares / width + 1e-05)[:, None]
    normed = (erased * inv_rms * norm_gain[None, :]).astype(jnp.bfloat16)

    per_t_seq = seq_rows // n_ten
    halves_n = _pick_chunks(per_t_seq, batch_count, n_sec)
    span = per_t_seq // halves_n
    part_rows = span * batch_count // n_sec
    grouped = normed.reshape(n_ten, halves_n, n_sec, part_rows, width_local)
    grouped = grouped.transpose(1, 2, 0, 3, 4)
    block_rows = n_ten * part_rows
    cols_n = _COLS if hidden_local % (_COLS * 128) == 0 else 1
    cols = hidden_local // cols_n

    def front(rows, cut):
        gate_c = jnp.dot(rows, gate_weight[:, cut], preferred_element_type=jnp.float32)
        up_c = jnp.dot(rows, up_weight[:, cut], preferred_element_type=jnp.float32)
        cur = jnp.concatenate([gate_c.astype(jnp.bfloat16), up_c.astype(jnp.bfloat16)], axis=-1)
        made = cur
        cur = cur.reshape(n_sec, block_rows, 2 * cols)
        first = None
        for bit in range(stages):
            halves = cur.reshape(cur.shape[0] // 2, 2, block_rows, 2 * cols)
            mine = (sec >> bit) & 1
            keep = lax.dynamic_index_in_dim(halves, mine, 1, keepdims=False)
            send = lax.dynamic_index_in_dim(halves, 1 - mine, 1, keepdims=False)
            if bit == stages - 1:
                first = send
            got = _swap(send, "section", n_sec, bit)
            cur = keep.astype(jnp.float32) + got.astype(jnp.float32)
            if bit < stages - 1:
                cur = cur.astype(jnp.bfloat16)
        return cur[0], made, first

    def back_a(cur):
        hid = (jax.nn.silu(cur[:, :cols]) * cur[:, cols:]).astype(jnp.bfloat16)
        cur = hid[None]
        return cur, _swap(cur, "section", n_sec, stages - 1)

    def join(cur, got, bit):
        first_mine = ((sec >> bit) & 1) == 0
        low = jnp.where(first_mine, cur, got)
        high = jnp.where(first_mine, got, cur)
        return jnp.stack([low, high], axis=1).reshape(2 * cur.shape[0], block_rows, cols)

    def back_b(cur, got):
        cur = join(cur, got, stages - 1)
        for bit in reversed(range(stages - 1)):
            cur = join(cur, _swap(cur, "section", n_sec, bit), bit)
        return cur.reshape(n_sec, n_ten, part_rows, cols)

    def finish(hid_parts):
        hid_all = jnp.concatenate(hid_parts, axis=-1).reshape(-1, hidden_local)
        acc = jnp.dot(hid_all, down_weight, preferred_element_type=jnp.float32)
        return acc.astype(jnp.bfloat16).reshape(n_sec, n_ten, part_rows, width_local)

    def scatter(down_h):
        bits = list(range(_stages(n_ten)))
        other = bits[1:2] + bits[:1] + bits[2:]
        half_w = width_local // 2
        piece = jnp.concatenate(
            [
                _scatter_sum(down_h[..., :half_w], "tensor", n_ten, bits, ten),
                _scatter_sum(down_h[..., half_w:], "tensor", n_ten, other, ten),
            ],
            axis=-1,
        )
        return piece.reshape(n_sec, part_rows, width_local)

    plan = [(h, c) for h in range(halves_n) for c in range(cols_n)]
    hid_parts = [[] for _ in range(halves_n)]
    downs = [None] * halves_n
    pending = None
    waiting = []
    sent = None

    def land(made):
        prev_h, cur, got = waiting.pop(0)
        if made is not None:
            got, _ = lax.optimization_barrier((got, made))
        hid_parts[prev_h].append(back_b(cur, got))
        if len(hid_parts[prev_h]) == cols_n:
            downs[prev_h] = finish(hid_parts[prev_h])

    for h, c in plan:
        rows = grouped[h].reshape(n_sec * block_rows, width_local)
        if sent is not None:
            rows, _ = lax.optimization_barrier((rows, sent))
        if h > 0 and c == cols_n - 1 and downs[h - 1] is not None:
            rows, _ = lax.optimization_barrier((rows, downs[h - 1]))
        reduced, made, sent = front(rows, slice(c * cols, (c + 1) * cols))
        if len(waiting) == 1:
            land(made)
        if pending is not None:
            prev_h, prev = pending
            prev, _ = lax.optimization_barrier((prev, made))
            waiting.append((prev_h,) + back_a(prev))
        pending = (h, reduced)
    prev_h, prev = pending
    done_downs = tuple(d for d in downs[:prev_h] if d is not None)
    if done_downs:
        prev, _ = lax.optimization_barrier((prev, done_downs))
    waiting.append((prev_h,) + back_a(prev))
    while waiting:
        land(None)
    pieces = [scatter(down_h) for down_h in downs]
    mixed = jnp.stack(pieces)
    mixed = mixed.reshape(per_t_seq, batch_count, width_local).astype(jnp.float32)
    own_rows = per_t_seq * batch_count
    erased_own = lax.dynamic_slice_in_dim(erased, ten * own_rows, own_rows, 0)
    erased_own = erased_own.reshape(per_t_seq, batch_count, width_local)
    return (erased_own + mixed).astype(jnp.bfloat16)


def solution(mesh):
    in_specs = (
        P(None, None, "section"),
        P("section"),
        P("section", None),
        P("section", None),
        P("section"),
        P("section", "tensor"),
        P("section", "tensor"),
        P("tensor", "section"),
    )
    out_specs = P("tensor", None, "section")
    return jax.shard_map(body, mesh=mesh, in_specs=in_specs, out_specs=out_specs, check_vma=False)
```

```python
import jax
import jax.numpy as jnp
from jax import lax
from jax.sharding import PartitionSpec as P


_COLS = 4


def _stages(n):
    count = n.bit_length() - 1
    assert 1 << count == n
    return count


def _swap(x, axis, n, bit):
    return lax.ppermute(x, axis, perm=[(a, a ^ (1 << bit)) for a in range(n)])


def _all_sum(x, axis, n):
    for bit in range(_stages(n)):
        x = x + _swap(x, axis, n, bit)
    return x


def _scatter_sum(x, axis, n, bit_order, me):
    count = _stages(n)
    blocks = x.reshape(x.shape[:1] + (2,) * count + x.shape[2:])
    for bit in bit_order:
        pos = 1 + count - 1 - bit
        pos = pos - sum(1 for done in bit_order[: bit_order.index(bit)] if done > bit)
        mine = (me >> bit) & 1
        keep = lax.dynamic_index_in_dim(blocks, mine, pos, keepdims=False)
        send = lax.dynamic_index_in_dim(blocks, 1 - mine, pos, keepdims=False)
        got = _swap(send.astype(jnp.bfloat16), axis, n, bit)
        blocks = keep.astype(jnp.float32) + got.astype(jnp.float32)
        if bit != bit_order[-1]:
            blocks = blocks.astype(jnp.bfloat16)
    return blocks


def _pick_chunks(per_t_seq, batch, n_sec):
    for k in (2, 1):
        if per_t_seq % k == 0 and (per_t_seq // k * batch) % n_sec == 0:
            return k
    raise ValueError("no chunking")


def body(
    stream, concept_mean, erase_basis, erase_lift, norm_gain, gate_weight, up_weight, down_weight
):
    seq_rows, batch_count, width_local = stream.shape
    n_sec = lax.axis_size("section")
    n_ten = lax.axis_size("tensor")
    stages = _stages(n_sec)
    sec = lax.axis_index("section")
    ten = lax.axis_index("tensor")
    width = width_local * n_sec
    hidden_local = gate_weight.shape[1]

    local_rows = stream.reshape(seq_rows * batch_count, width_local)
    partial_basis = jnp.dot(local_rows, erase_basis, preferred_element_type=jnp.float32)
    partial_mean = jnp.dot(concept_mean, erase_basis, preferred_element_type=jnp.float32)
    totals = _all_sum(jnp.concatenate([partial_basis, partial_mean[None, :]], axis=0), "section", n_sec)
    coords = totals[:-1] - totals[-1:]
    lift_float = erase_lift.astype(jnp.float32)
    erased = local_rows.astype(jnp.float32) - jnp.dot(
        coords, lift_float.T, precision=lax.Precision.HIGHEST
    )
    squares = _all_sum(jnp.sum(erased * erased, axis=-1), "section", n_sec)
    inv_rms = lax.rsqrt(squares / width + 1e-05)[:, None]
    normed = (erased * inv_rms * norm_gain[None, :]).astype(jnp.bfloat16)

    per_t_seq = seq_rows // n_ten
    halves_n = _pick_chunks(per_t_seq, batch_count, n_sec)
    span = per_t_seq // halves_n
    part_rows = span * batch_count // n_sec
    grouped = normed.reshape(n_ten, halves_n, n_sec, part_rows, width_local)
    grouped = grouped.transpose(1, 2, 0, 3, 4)
    block_rows = n_ten * part_rows
    cols_n = _COLS if hidden_local % (_COLS * 128) == 0 else 1
    cols = hidden_local // cols_n

    def front(rows, cut):
        gate_c = jnp.dot(rows, gate_weight[:, cut], preferred_element_type=jnp.float32)
        up_c = jnp.dot(rows, up_weight[:, cut], preferred_element_type=jnp.float32)
        cur = jnp.concatenate([gate_c.astype(jnp.bfloat16), up_c.astype(jnp.bfloat16)], axis=-1)
        made = cur
        cur = cur.reshape(n_sec, block_rows, 2 * cols)
        first = None
        for bit in range(stages):
            halves = cur.reshape(cur.shape[0] // 2, 2, block_rows, 2 * cols)
            mine = (sec >> bit) & 1
            keep = lax.dynamic_index_in_dim(halves, mine, 1, keepdims=False)
            send = lax.dynamic_index_in_dim(halves, 1 - mine, 1, keepdims=False)
            if bit == stages - 1:
                first = send
            got = _swap(send, "section", n_sec, bit)
            cur = keep.astype(jnp.float32) + got.astype(jnp.float32)
            if bit < stages - 1:
                cur = cur.astype(jnp.bfloat16)
        return cur[0], made, first

    def back_a(cur):
        hid = (jax.nn.silu(cur[:, :cols]) * cur[:, cols:]).astype(jnp.bfloat16)
        cur = hid[None]
        return cur, _swap(cur, "section", n_sec, stages - 1)

    def join(cur, got, bit):
        first_mine = ((sec >> bit) & 1) == 0
        low = jnp.where(first_mine, cur, got)
        high = jnp.where(first_mine, got, cur)
        return jnp.stack([low, high], axis=1).reshape(2 * cur.shape[0], block_rows, cols)

    def back_b(cur, got):
        cur = join(cur, got, stages - 1)
        for bit in reversed(range(stages - 1)):
            cur = join(cur, _swap(cur, "section", n_sec, bit), bit)
        return cur.reshape(n_sec, n_ten, part_rows, cols)

    def finish(hid_parts):
        hid_all = jnp.concatenate(hid_parts, axis=-1).reshape(-1, hidden_local)
        acc = jnp.dot(hid_all, down_weight, preferred_element_type=jnp.float32)
        return acc.astype(jnp.bfloat16).reshape(n_sec, n_ten, part_rows, width_local)

    def scatter(down_h):
        bits = list(range(_stages(n_ten)))
        other = bits[1:2] + bits[:1] + bits[2:]
        half_w = width_local // 2
        piece = jnp.concatenate(
            [
                _scatter_sum(down_h[..., :half_w], "tensor", n_ten, bits, ten),
                _scatter_sum(down_h[..., half_w:], "tensor", n_ten, other, ten),
            ],
            axis=-1,
        )
        return piece.reshape(n_sec, part_rows, width_local)

    plan = [(h, c) for h in range(halves_n) for c in range(cols_n)]
    hid_parts = [[] for _ in range(halves_n)]
    downs = [None] * halves_n
    pending = None
    waiting = []
    sent = None

    def land(made):
        prev_h, cur, got = waiting.pop(0)
        if made is not None:
            got, _ = lax.optimization_barrier((got, made))
        hid_parts[prev_h].append(back_b(cur, got))
        if len(hid_parts[prev_h]) == cols_n:
            downs[prev_h] = finish(hid_parts[prev_h])

    for h, c in plan:
        rows = grouped[h].reshape(n_sec * block_rows, width_local)
        if sent is not None:
            rows, _ = lax.optimization_barrier((rows, sent))
        if h > 0 and c == cols_n - 1 and downs[h - 1] is not None:
            rows, _ = lax.optimization_barrier((rows, downs[h - 1]))
        reduced, made, sent = front(rows, slice(c * cols, (c + 1) * cols))
        if len(waiting) == 1:
            land(made)
        if pending is not None:
            prev_h, prev = pending
            prev, _ = lax.optimization_barrier((prev, made))
            waiting.append((prev_h,) + back_a(prev))
        pending = (h, reduced)
    prev_h, prev = pending
    done_downs = tuple(d for d in downs[:prev_h] if d is not None)
    if done_downs:
        prev, _ = lax.optimization_barrier((prev, done_downs))
    waiting.append((prev_h,) + back_a(prev))
    while waiting:
        land(None)
    pieces = [scatter(down_h) for down_h in downs]
    mixed = jnp.stack(pieces)
    mixed = mixed.reshape(per_t_seq, batch_count, width_local).astype(jnp.float32)
    own_rows = per_t_seq * batch_count
    erased_own = lax.dynamic_slice_in_dim(erased, ten * own_rows, own_rows, 0)
    erased_own = erased_own.reshape(per_t_seq, batch_count, width_local)
    return (erased_own + mixed).astype(jnp.bfloat16)


def solution(mesh):
    in_specs = (
        P(None, None, "section"),
        P("section"),
        P("section", None),
        P("section", None),
        P("section"),
        P("section", "tensor"),
        P("section", "tensor"),
        P("tensor", "section"),
    )
    out_specs = P("tensor", None, "section")
    return jax.shard_map(body, mesh=mesh, in_specs=in_specs, out_specs=out_specs, check_vma=False)
```

```python
import jax
import jax.numpy as jnp
from jax import lax
from jax.sharding import PartitionSpec as P


_COLS = 2


def _stages(n):
    count = n.bit_length() - 1
    assert 1 << count == n
    return count


def _swap(x, axis, n, bit):
    return lax.ppermute(x, axis, perm=[(a, a ^ (1 << bit)) for a in range(n)])


def _all_sum(x, axis, n):
    for bit in range(_stages(n)):
        x = x + _swap(x, axis, n, bit)
    return x


def _scatter_sum(x, axis, n, bit_order, me):
    count = _stages(n)
    blocks = x.reshape(x.shape[:1] + (2,) * count + x.shape[2:])
    for bit in bit_order:
        pos = 1 + count - 1 - bit
        pos = pos - sum(1 for done in bit_order[: bit_order.index(bit)] if done > bit)
        mine = (me >> bit) & 1
        keep = lax.dynamic_index_in_dim(blocks, mine, pos, keepdims=False)
        send = lax.dynamic_index_in_dim(blocks, 1 - mine, pos, keepdims=False)
        got = _swap(send.astype(jnp.bfloat16), axis, n, bit)
        blocks = keep.astype(jnp.float32) + got.astype(jnp.float32)
        if bit != bit_order[-1]:
            blocks = blocks.astype(jnp.bfloat16)
    return blocks


def _all_sum_narrow(x, axis, n):
    for bit in range(_stages(n)):
        sent = x.astype(jnp.bfloat16)
        x = sent.astype(jnp.float32) + _swap(sent, axis, n, bit).astype(jnp.float32)
    return x


def _pick_chunks(per_t_seq, batch, n_sec):
    for k in (2, 1):
        if per_t_seq % k == 0 and (per_t_seq // k * batch) % n_sec == 0:
            return k
    raise ValueError("no chunking")


def body(
    stream, concept_mean, erase_basis, erase_lift, norm_gain, gate_weight, up_weight, down_weight
):
    seq_rows, batch_count, width_local = stream.shape
    n_sec = lax.axis_size("section")
    n_ten = lax.axis_size("tensor")
    stages = _stages(n_sec)
    sec = lax.axis_index("section")
    ten = lax.axis_index("tensor")
    width = width_local * n_sec
    hidden_local = gate_weight.shape[1]

    local_rows = stream.reshape(seq_rows * batch_count, width_local)
    partial_basis = jnp.dot(local_rows, erase_basis, preferred_element_type=jnp.float32)
    partial_mean = jnp.dot(concept_mean, erase_basis, preferred_element_type=jnp.float32)
    totals = _all_sum_narrow(
        jnp.concatenate([partial_basis, partial_mean[None, :]], axis=0), "section", n_sec
    )
    coords = totals[:-1] - totals[-1:]
    lift_float = erase_lift.astype(jnp.float32)
    erased = local_rows.astype(jnp.float32) - jnp.dot(
        coords, lift_float.T, precision=lax.Precision.HIGHEST
    )
    squares = _all_sum(jnp.sum(erased * erased, axis=-1), "section", n_sec)
    inv_rms = lax.rsqrt(squares / width + 1e-05)[:, None]
    normed = (erased * inv_rms * norm_gain[None, :]).astype(jnp.bfloat16)

    per_t_seq = seq_rows // n_ten
    halves_n = _pick_chunks(per_t_seq, batch_count, n_sec)
    span = per_t_seq // halves_n
    part_rows = span * batch_count // n_sec
    grouped = normed.reshape(n_ten, halves_n, n_sec, part_rows, width_local)
    grouped = grouped.transpose(1, 2, 0, 3, 4)
    block_rows = n_ten * part_rows
    cols_n = _COLS if hidden_local % (_COLS * 128) == 0 else 1
    cols = hidden_local // cols_n

    def front(rows, cut):
        gate_c = jnp.dot(rows, gate_weight[:, cut], preferred_element_type=jnp.float32)
        up_c = jnp.dot(rows, up_weight[:, cut], preferred_element_type=jnp.float32)
        cur = jnp.concatenate([gate_c.astype(jnp.bfloat16), up_c.astype(jnp.bfloat16)], axis=-1)
        made = cur
        cur = cur.reshape(n_sec, block_rows, 2 * cols)
        first = None
        for bit in range(stages):
            halves = cur.reshape(cur.shape[0] // 2, 2, block_rows, 2 * cols)
            mine = (sec >> bit) & 1
            keep = lax.dynamic_index_in_dim(halves, mine, 1, keepdims=False)
            send = lax.dynamic_index_in_dim(halves, 1 - mine, 1, keepdims=False)
            if bit == stages - 1:
                first = send
            got = _swap(send, "section", n_sec, bit)
            cur = keep.astype(jnp.float32) + got.astype(jnp.float32)
            if bit < stages - 1:
                cur = cur.astype(jnp.bfloat16)
        return cur[0], made, first

    def back_a(cur):
        hid = (jax.nn.silu(cur[:, :cols]) * cur[:, cols:]).astype(jnp.bfloat16)
        cur = hid[None]
        return cur, _swap(cur, "section", n_sec, stages - 1)

    def join(cur, got, bit):
        first_mine = ((sec >> bit) & 1) == 0
        low = jnp.where(first_mine, cur, got)
        high = jnp.where(first_mine, got, cur)
        return jnp.stack([low, high], axis=1).reshape(2 * cur.shape[0], block_rows, cols)

    def back_b(cur, got):
        cur = join(cur, got, stages - 1)
        for bit in reversed(range(stages - 1)):
            cur = join(cur, _swap(cur, "section", n_sec, bit), bit)
        return cur.reshape(n_sec, n_ten, part_rows, cols)

    def finish(hid_parts):
        hid_all = jnp.concatenate(hid_parts, axis=-1).reshape(-1, hidden_local)
        acc = jnp.dot(hid_all, down_weight, preferred_element_type=jnp.float32)
        return acc.astype(jnp.bfloat16).reshape(n_sec, n_ten, part_rows, width_local)

    def scatter(down_h):
        bits = list(range(_stages(n_ten)))
        other = bits[1:2] + bits[:1] + bits[2:]
        half_w = width_local // 2
        piece = jnp.concatenate(
            [
                _scatter_sum(down_h[..., :half_w], "tensor", n_ten, bits, ten),
                _scatter_sum(down_h[..., half_w:], "tensor", n_ten, other, ten),
            ],
            axis=-1,
        )
        return piece.reshape(n_sec, part_rows, width_local)

    plan = [(h, c) for h in range(halves_n) for c in range(cols_n)]
    hid_parts = [[] for _ in range(halves_n)]
    downs = [None] * halves_n
    pending = None
    waiting = []
    sent = None

    def land(made):
        prev_h, cur, got = waiting.pop(0)
        if made is not None:
            got, _ = lax.optimization_barrier((got, made))
        hid_parts[prev_h].append(back_b(cur, got))
        if len(hid_parts[prev_h]) == cols_n:
            downs[prev_h] = finish(hid_parts[prev_h])

    for h, c in plan:
        rows = grouped[h].reshape(n_sec * block_rows, width_local)
        if sent is not None:
            rows, _ = lax.optimization_barrier((rows, sent))
        if h > 0 and c == cols_n - 1 and downs[h - 1] is not None:
            rows, _ = lax.optimization_barrier((rows, downs[h - 1]))
        reduced, made, sent = front(rows, slice(c * cols, (c + 1) * cols))
        if len(waiting) == 1:
            land(made)
        if pending is not None:
            prev_h, prev = pending
            prev, _ = lax.optimization_barrier((prev, made))
            waiting.append((prev_h,) + back_a(prev))
        pending = (h, reduced)
    prev_h, prev = pending
    done_downs = tuple(d for d in downs[:prev_h] if d is not None)
    if done_downs:
        prev, _ = lax.optimization_barrier((prev, done_downs))
    waiting.append((prev_h,) + back_a(prev))
    while waiting:
        land(None)
    pieces = [scatter(down_h) for down_h in downs]
    mixed = jnp.stack(pieces)
    mixed = mixed.reshape(per_t_seq, batch_count, width_local).astype(jnp.float32)
    own_rows = per_t_seq * batch_count
    erased_own = lax.dynamic_slice_in_dim(erased, ten * own_rows, own_rows, 0)
    erased_own = erased_own.reshape(per_t_seq, batch_count, width_local)
    return (erased_own + mixed).astype(jnp.bfloat16)


def solution(mesh):
    in_specs = (
        P(None, None, "section"),
        P("section"),
        P("section", None),
        P("section", None),
        P("section"),
        P("section", "tensor"),
        P("section", "tensor"),
        P("tensor", "section"),
    )
    out_specs = P("tensor", None, "section")
    return jax.shard_map(body, mesh=mesh, in_specs=in_specs, out_specs=out_specs, check_vma=False)
```

```python
import jax
import jax.numpy as jnp
from jax import lax
from jax.sharding import PartitionSpec as P


_COLS = 2


def _stages(n):
    count = n.bit_length() - 1
    assert 1 << count == n
    return count


def _swap(x, axis, n, bit):
    return lax.ppermute(x, axis, perm=[(a, a ^ (1 << bit)) for a in range(n)])


def _all_sum(x, axis, n):
    for bit in range(_stages(n)):
        x = x + _swap(x, axis, n, bit)
    return x


def _scatter_sum(x, axis, n, bit_order, me):
    count = _stages(n)
    blocks = x.reshape(x.shape[:1] + (2,) * count + x.shape[2:])
    for bit in bit_order:
        pos = 1 + count - 1 - bit
        pos = pos - sum(1 for done in bit_order[: bit_order.index(bit)] if done > bit)
        mine = (me >> bit) & 1
        keep = lax.dynamic_index_in_dim(blocks, mine, pos, keepdims=False)
        send = lax.dynamic_index_in_dim(blocks, 1 - mine, pos, keepdims=False)
        got = _swap(send.astype(jnp.bfloat16), axis, n, bit)
        blocks = keep.astype(jnp.float32) + got.astype(jnp.float32)
        if bit != bit_order[-1]:
            blocks = blocks.astype(jnp.bfloat16)
    return blocks


def _all_sum_narrow(x, axis, n):
    for bit in range(_stages(n)):
        sent = x.astype(jnp.bfloat16)
        x = sent.astype(jnp.float32) + _swap(sent, axis, n, bit).astype(jnp.float32)
    return x


def _pick_chunks(per_t_seq, batch, n_sec):
    for k in (2, 1):
        if per_t_seq % k == 0 and (per_t_seq // k * batch) % n_sec == 0:
            return k
    raise ValueError("no chunking")


def body(
    stream, concept_mean, erase_basis, erase_lift, norm_gain, gate_weight, up_weight, down_weight
):
    seq_rows, batch_count, width_local = stream.shape
    n_sec = lax.axis_size("section")
    n_ten = lax.axis_size("tensor")
    stages = _stages(n_sec)
    sec = lax.axis_index("section")
    ten = lax.axis_index("tensor")
    width = width_local * n_sec
    hidden_local = gate_weight.shape[1]

    partial_basis = jnp.einsum(
        "sbd,dr->sbr", stream, erase_basis, preferred_element_type=jnp.float32
    ).reshape(seq_rows * batch_count, -1)
    partial_mean = jnp.dot(concept_mean, erase_basis, preferred_element_type=jnp.float32)
    totals = _all_sum_narrow(
        jnp.concatenate([partial_basis, partial_mean[None, :]], axis=0), "section", n_sec
    )
    coords = (totals[:-1] - totals[-1:]).reshape(seq_rows, batch_count, -1)
    lift_float = erase_lift.astype(jnp.float32)
    erased = stream.astype(jnp.float32) - jnp.einsum(
        "sbr,dr->sbd", coords, lift_float, precision=lax.Precision.HIGHEST
    )
    squares = _all_sum(jnp.sum(erased * erased, axis=-1), "section", n_sec)
    inv_rms = lax.rsqrt(squares / width + 1e-05)[:, :, None]
    normed = (erased * inv_rms * norm_gain[None, None, :]).astype(jnp.bfloat16)

    per_t_seq = seq_rows // n_ten
    halves_n = _pick_chunks(per_t_seq, batch_count, n_sec)
    span = per_t_seq // halves_n
    part_rows = span * batch_count // n_sec
    grouped = normed.reshape(n_ten, halves_n, n_sec, part_rows, width_local)
    grouped = grouped.transpose(1, 2, 0, 3, 4)
    block_rows = n_ten * part_rows
    cols_n = _COLS if hidden_local % (_COLS * 128) == 0 else 1
    cols = hidden_local // cols_n

    def front(rows, cut):
        gate_c = jnp.dot(rows, gate_weight[:, cut], preferred_element_type=jnp.float32)
        up_c = jnp.dot(rows, up_weight[:, cut], preferred_element_type=jnp.float32)
        cur = jnp.concatenate([gate_c.astype(jnp.bfloat16), up_c.astype(jnp.bfloat16)], axis=-1)
        made = cur
        cur = cur.reshape(n_sec, block_rows, 2 * cols)
        first = None
        for bit in range(stages):
            halves = cur.reshape(cur.shape[0] // 2, 2, block_rows, 2 * cols)
            mine = (sec >> bit) & 1
            keep = lax.dynamic_index_in_dim(halves, mine, 1, keepdims=False)
            send = lax.dynamic_index_in_dim(halves, 1 - mine, 1, keepdims=False)
            if bit == stages - 1:
                first = send
            got = _swap(send, "section", n_sec, bit)
            cur = keep.astype(jnp.float32) + got.astype(jnp.float32)
            if bit < stages - 1:
                cur = cur.astype(jnp.bfloat16)
        return cur[0], made, first

    def back_a(cur):
        hid = (jax.nn.silu(cur[:, :cols]) * cur[:, cols:]).astype(jnp.bfloat16)
        cur = hid[None]
        return cur, _swap(cur, "section", n_sec, stages - 1)

    def join(cur, got, bit):
        first_mine = ((sec >> bit) & 1) == 0
        low = jnp.where(first_mine, cur, got)
        high = jnp.where(first_mine, got, cur)
        return jnp.stack([low, high], axis=1).reshape(2 * cur.shape[0], block_rows, cols)

    def back_b(cur, got):
        cur = join(cur, got, stages - 1)
        for bit in reversed(range(stages - 1)):
            cur = join(cur, _swap(cur, "section", n_sec, bit), bit)
        return cur.reshape(n_sec, n_ten, part_rows, cols)

    def finish(hid_parts):
        hid_all = jnp.concatenate(hid_parts, axis=-1).reshape(-1, hidden_local)
        acc = jnp.dot(hid_all, down_weight, preferred_element_type=jnp.float32)
        return acc.astype(jnp.bfloat16).reshape(n_sec, n_ten, part_rows, width_local)

    def scatter(down_h):
        bits = list(range(_stages(n_ten)))
        other = bits[1:2] + bits[:1] + bits[2:]
        half_w = width_local // 2
        piece = jnp.concatenate(
            [
                _scatter_sum(down_h[..., :half_w], "tensor", n_ten, bits, ten),
                _scatter_sum(down_h[..., half_w:], "tensor", n_ten, other, ten),
            ],
            axis=-1,
        )
        return piece.reshape(n_sec, part_rows, width_local)

    plan = [(h, c) for h in range(halves_n) for c in range(cols_n)]
    hid_parts = [[] for _ in range(halves_n)]
    downs = [None] * halves_n
    pending = None
    waiting = []
    sent = None

    def land(made):
        prev_h, cur, got = waiting.pop(0)
        if made is not None:
            got, _ = lax.optimization_barrier((got, made))
        hid_parts[prev_h].append(back_b(cur, got))
        if len(hid_parts[prev_h]) == cols_n:
            downs[prev_h] = finish(hid_parts[prev_h])

    for h, c in plan:
        rows = grouped[h].reshape(n_sec * block_rows, width_local)
        if sent is not None:
            rows, _ = lax.optimization_barrier((rows, sent))
        if h > 0 and c == cols_n - 1 and downs[h - 1] is not None:
            rows, _ = lax.optimization_barrier((rows, downs[h - 1]))
        reduced, made, sent = front(rows, slice(c * cols, (c + 1) * cols))
        if len(waiting) == 1:
            land(made)
        if pending is not None:
            prev_h, prev = pending
            prev, _ = lax.optimization_barrier((prev, made))
            waiting.append((prev_h,) + back_a(prev))
        pending = (h, reduced)
    prev_h, prev = pending
    done_downs = tuple(d for d in downs[:prev_h] if d is not None)
    if done_downs:
        prev, _ = lax.optimization_barrier((prev, done_downs))
    waiting.append((prev_h,) + back_a(prev))
    while waiting:
        land(None)
    pieces = [scatter(down_h) for down_h in downs]
    mixed = jnp.stack(pieces)
    mixed = mixed.reshape(per_t_seq, batch_count, width_local).astype(jnp.float32)
    erased_own = lax.dynamic_slice_in_dim(erased, ten * per_t_seq, per_t_seq, 0)
    return (erased_own + mixed).astype(jnp.bfloat16)


def solution(mesh):
    in_specs = (
        P(None, None, "section"),
        P("section"),
        P("section", None),
        P("section", None),
        P("section"),
        P("section", "tensor"),
        P("section", "tensor"),
        P("tensor", "section"),
    )
    out_specs = P("tensor", None, "section")
    return jax.shard_map(body, mesh=mesh, in_specs=in_specs, out_specs=out_specs, check_vma=False)
```
